512 devices in a mesh: dp: 128 (over z, x, core), head: 4 (over y).
Axes of the slice: x: 4, y: 4, z: 16, core: 2. Of those that a mesh axis runs over, the one named last changes fastest.
Arguments:
- queries: bfloat16 [2, 1536, 8192], P(None, 'dp', 'head'), may hold values from -180 to 180
- new_kv: bfloat16 [2, 2, 1536, 512], P(None, None, 'dp', 'head'), may hold values from -6 to 6
- cache: bfloat16 [2, 1536, 64, 512], P(None, 'dp', None, 'head'), may hold values from -9 to 9
- lengths: int32 [1536], P('dp'), may hold values from 2 to 64, as said below
- positions: int32 [2, 3, 1536], P(None, None, 'dp'), may hold values from 0 to 4095
- hidden: bfloat16 [2, 1536, 4096], P(None, 'dp', 'head'), may hold values from -6 to 6
- norm_gain: bfloat16 [4096], replicated, may hold values from 0.5 to 1.5
- route_ids: int32 [2, 1536, 8], P(None, 'dp'), may hold values from 0 to 127, as said below
- route_weight: float32 [2, 1536, 8], P(None, 'dp'), may hold values from 0.05 to 1
- w_gate_up: bfloat16 [128, 4096, 1536], P('dp', None, 'head'), may hold values from -0.09375 to 0.09375
- w_down: bfloat16 [128, 768, 4096], P('dp', 'head'), may hold values from -0.21875 to 0.21875
Outputs:
- attention: bfloat16 [2, 1536, 8192], P(None, 'dp', 'head')
- layer_out: bfloat16 [2, 1536, 4096], P(None, 'dp', 'head')
The draws below stay inside these ranges and needn't reach their ends.
Inputs may be any that keep to these rules, and one draw needn't show every extreme that they name: `route_ids`: each token names 8 different experts. Among the rows of one index of dp in one step no expert is named more than 2 times, and in each step some expert is named exactly 2 times by the rows of every index of dp. `lengths`: some request uses all 64 slots.
All inputs are finite; a program needn't handle non-finite values.
Results may differ from the reference program's by a relative error of at most 0.012.
The reference program's roundings to bfloat16 on the way count: a program that leaves them out, or rounds other values in their place, can miss the bound.
Values may be sent and summed in bfloat16 or wider, within the bound.
No kernel may reach another device: no remote copies, remote signals or barrier semaphores. Data moves between devices by JAX's collectives and lax.ppermute only.
A program may use at most 64 MiB of HBM per device.

```python
import math
import jax
import jax.numpy as jnp
from jax import lax

D = 4096
QH = 64
KVH = 4
HD = 128
TOPK = 8
FF = 768
STEPS = 2
R_DEV = 12
CACHE = 64
EXPERTS = 128
REQUESTS = 1536
S = 2
N_DP = 128
N_HEAD = 4


def position_table(key):
    return jax.random.randint(jax.random.fold_in(key, 101), (STEPS, 3, REQUESTS), 0, 4096, dtype=jnp.int32)


def length_table(key):
    first_key, second_key = jax.random.split(jax.random.fold_in(key, 102))
    drawn = jax.random.randint(first_key, (REQUESTS,), 2, CACHE + 1, dtype=jnp.int32)
    longest = jax.random.randint(second_key, (), 0, REQUESTS, dtype=jnp.int32)
    return jnp.where(jnp.arange(REQUESTS, dtype=jnp.int32) == longest, CACHE, drawn).astype(jnp.int32)


def fresh_pairs(key):
    drawn = jax.random.normal(jax.random.fold_in(key, 103), (STEPS, 2, REQUESTS, KVH * HD), jnp.float32)
    return jnp.clip(drawn, -6.0, 6.0)


def draw_positions(key, part):
    return position_table(key)


def draw_lengths(key, part):
    return length_table(key)


def draw_new_kv(key, part):
    return fresh_pairs(key).astype(jnp.bfloat16)


def draw_queries(key, part):
    drawn = jax.random.normal(jax.random.fold_in(key, 105), (STEPS, REQUESTS, QH * HD), jnp.float32)
    drawn = jnp.clip(drawn, -6.0, 6.0)
    return drawn.astype(jnp.bfloat16)


def draw_cache(key, part):
    drawn = jax.random.normal(jax.random.fold_in(key, 107), (2, REQUESTS, CACHE, KVH * HD), jnp.float32)
    drawn = jnp.clip(drawn, -6.0, 6.0)
    return drawn.astype(jnp.bfloat16)


def shuffle_one(key_one, count):
    return jax.random.permutation(key_one, count)


def partial_perm(count):

    def permute(key_one):
        return shuffle_one(key_one, count)
    return permute


def draw_route_ids(key, part):
    block_count = STEPS * (REQUESTS // R_DEV)
    key_hot, key_other, key_tokens, key_slots = jax.random.split(jax.random.fold_in(key, 108), 4)
    hot_expert = jax.random.randint(key_hot, (STEPS,), 0, EXPERTS, dtype=jnp.int32)
    hot_rows = jnp.repeat(hot_expert, REQUESTS // R_DEV)
    others = jax.vmap(partial_perm(EXPERTS - 1))(jax.random.split(key_other, block_count)).astype(jnp.int32)
    others = others + (others >= hot_rows[:, None]).astype(jnp.int32)
    spread = TOPK // 2
    listing = jnp.concatenate([others[:, :spread], hot_rows[:, None], others[:, spread:]], 1)
    picking = (jnp.arange(R_DEV, dtype=jnp.int32)[:, None] * spread + jnp.arange(TOPK, dtype=jnp.int32)[None, :]) % EXPERTS
    chosen_ids = listing[:, picking]
    token_order = jax.vmap(partial_perm(R_DEV))(jax.random.split(key_tokens, block_count)).astype(jnp.int32)
    chosen_ids = jnp.take_along_axis(chosen_ids, token_order[:, :, None], axis=1)
    slot_order = jax.vmap(partial_perm(TOPK))(jax.random.split(key_slots, block_count * R_DEV)).astype(jnp.int32)
    chosen_ids = jnp.take_along_axis(chosen_ids, slot_order.reshape(block_count, R_DEV, TOPK), axis=2)
    return chosen_ids.reshape(STEPS, REQUESTS, TOPK).astype(jnp.int32)


def levels(own_key, dims, pieces, low, top_value):
    level = 1.0
    for position, parts in pieces:
        steps = jax.random.uniform(jax.random.fold_in(jax.random.fold_in(own_key, 6), position), (parts,), jnp.float32, low / len(pieces), top_value / len(pieces))
        level = level * jnp.repeat(jnp.exp(steps), dims[position] // parts).reshape((-1,) + (1,) * (len(dims) - 1 - position))
    return level


def bell_draw(rng, dims, scale, bound, shards=(), held_as=jnp.bfloat16):
    result = scale * jax.random.normal(rng, dims, jnp.float32)
    if shards:
        result = result * levels(rng, dims, shards, -0.22, 0.18)
    return jnp.clip(result, -bound, bound).astype(held_as)


def setup_inputs(seed: int = 0) -> dict:
    splits = jax.random.split(jax.random.key(seed), 12)
    queries = draw_queries(jax.random.fold_in(splits[11], 71), 0)
    new_kv = draw_new_kv(jax.random.fold_in(splits[11], 71), 0)
    cache = draw_cache(jax.random.fold_in(splits[11], 71), 0)
    lengths = draw_lengths(jax.random.fold_in(splits[11], 71), 0)
    positions = draw_positions(jax.random.fold_in(splits[11], 71), 0)
    hidden = bell_draw(splits[5], (STEPS, REQUESTS, D), 1.0, 6.0, ((1, 128), (2, 4)))
    norm_gain = jnp.clip(1.0 + 0.1 * jax.random.normal(splits[6], (D,), jnp.float32), 0.5, 1.5).astype(jnp.bfloat16)
    route_ids = draw_route_ids(jax.random.fold_in(splits[11], 71), 0)
    route_weight = jnp.clip(jnp.exp(math.log(1.0) - 2.9957323 * jax.random.uniform(splits[8], (STEPS, REQUESTS, TOPK), jnp.float32) ** levels(splits[8], (STEPS, REQUESTS, TOPK), ((1, 128),), -0.2, 0.2)), 0.05, 1.0)
    w_gate_up = bell_draw(splits[9], (EXPERTS, D, 2 * FF), D ** -0.5, 0.09375, ((0, 128), (2, 4)))
    w_down = bell_draw(splits[10], (EXPERTS, FF, D), FF ** -0.5, 0.21875, ((0, 128), (1, 4)))
    return {"queries": queries, "new_kv": new_kv, "cache": cache, "lengths": lengths, "positions": positions, "hidden": hidden, "norm_gain": norm_gain, "route_ids": route_ids, "route_weight": route_weight, "w_gate_up": w_gate_up, "w_down": w_down}


EPS = 1e-06
ROPE_BASE = 5000000.0

def rotate(vectors, pos_ids):
    head_size = vectors.shape[-1]
    half_dim = head_size // 2
    freq_index = jnp.arange(half_dim, dtype=jnp.int32)
    inverse_freq = jnp.exp(freq_index.astype(jnp.float32) * (-2.0 * math.log(ROPE_BASE) / head_size))
    alternated = 60 * half_dim // 64
    axis_pick = jnp.where(freq_index < alternated, freq_index % 3, 0)
    pos_float = pos_ids.astype(jnp.float32)
    chosen = jnp.where(axis_pick[None, :] == 0, pos_float[0][:, None], jnp.where(axis_pick[None, :] == 1, pos_float[1][:, None], pos_float[2][:, None]))
    angles = chosen * inverse_freq[None, :]
    cosine = jnp.cos(angles)[:, None, :]
    sine_part = jnp.sin(angles)[:, None, :]
    first_half = vectors[..., :half_dim]
    second_half = vectors[..., half_dim:]
    return jnp.concatenate([first_half * cosine - second_half * sine_part, second_half * cosine + first_half * sine_part], -1)

def rounded(values):
    return lax.optimization_barrier(values.astype(jnp.bfloat16)).astype(jnp.float32)

def expert_layer(normed, route_step, shares, w_gate_up, w_down):
    flat_ids = route_step.reshape(-1)
    flat_shares = shares.reshape(-1)
    capacity = S * N_DP
    hidden_part = FF // N_HEAD

    def per_expert(total, expert):
        hit = flat_ids == expert
        order = jnp.argsort(jnp.where(hit, 0, 1).astype(jnp.int32), stable=True)[:capacity]
        tokens = (order // TOPK).astype(jnp.int32)
        weight = jnp.where(hit[order], flat_shares[order], 0.0)
        rows = normed[tokens]
        arranged = w_gate_up[expert].reshape(D, N_HEAD, 2, hidden_part)
        gate_cols = arranged[:, :, 0, :].reshape(D, FF)
        up_cols = arranged[:, :, 1, :].reshape(D, FF)
        gate_val = jnp.dot(rows, gate_cols, preferred_element_type=jnp.float32)
        up_val = jnp.dot(rows, up_cols, preferred_element_type=jnp.float32)
        activated = (jax.nn.silu(gate_val) * up_val).astype(jnp.bfloat16)
        partial_out = jnp.einsum('cqf,qfd->qcd', activated.reshape(capacity, N_HEAD, hidden_part).astype(jnp.float32), w_down[expert].reshape(N_HEAD, hidden_part, D).astype(jnp.float32))
        merged = lax.optimization_barrier(jnp.sum(rounded(partial_out), 0))
        return (total.at[tokens].add(weight[:, None] * merged), None)
    total, _ = lax.scan(per_expert, jnp.zeros((REQUESTS, D), jnp.float32), jnp.arange(EXPERTS, dtype=jnp.int32))
    return total

def reference(queries, new_kv, cache, lengths, positions, hidden, norm_gain, route_ids, route_weight, w_gate_up, w_down):
    group = QH // KVH
    score_scale = 1.0 / math.sqrt(HD)
    fresh_keys = jnp.stack([rounded(rotate(new_kv[step_at, 0].reshape(REQUESTS, KVH, HD).astype(jnp.float32), positions[step_at])) for step_at in range(STEPS)], 0)
    fresh_values = new_kv[:, 1].reshape(STEPS, REQUESTS, KVH, HD).astype(jnp.float32)
    cache_keys = cache[0].reshape(REQUESTS, CACHE, KVH, HD).astype(jnp.float32)
    cache_values = cache[1].reshape(REQUESTS, CACHE, KVH, HD).astype(jnp.float32)
    usable = jnp.arange(CACHE, dtype=jnp.int32)[None, :] < lengths[:, None]
    attention = []
    for step_at in range(STEPS):
        rotated_q = rounded(rotate(queries[step_at].reshape(REQUESTS, QH, HD).astype(jnp.float32), positions[step_at]))
        rotated_q = rotated_q.reshape(REQUESTS, KVH, group, HD)
        cached = jnp.einsum('rkgd,rlkd->rkgl', rotated_q, cache_keys) * score_scale
        cached = jnp.where(usable[:, None, None, :], cached, -1e+30)
        recent = jnp.einsum('rkgd,nrkd->rkgn', rotated_q, fresh_keys[:step_at + 1]) * score_scale
        scores = jnp.concatenate([cached, recent], -1)
        row_max = lax.optimization_barrier(jnp.max(scores, -1, keepdims=True))
        shifted = jnp.exp(scores - row_max)
        weights = rounded(shifted / lax.optimization_barrier(jnp.sum(shifted, -1, keepdims=True)))
        mixture = jnp.einsum('rkgl,rlkd->rkgd', weights[..., :CACHE], cache_values)
        mixture = mixture + jnp.einsum('rkgn,nrkd->rkgd', weights[..., CACHE:], fresh_values[:step_at + 1])
        attention.append(mixture.astype(jnp.bfloat16).reshape(REQUESTS, QH * HD))
    layers = []
    for step_at in range(STEPS):
        residual = hidden[step_at].astype(jnp.float32)
        mean_sq = lax.optimization_barrier(jnp.mean(residual * residual, -1, keepdims=True))
        normed = (residual * lax.rsqrt(mean_sq + EPS) * norm_gain).astype(jnp.bfloat16)
        shares = route_weight[step_at] / lax.optimization_barrier(jnp.sum(route_weight[step_at], -1, keepdims=True))
        total = expert_layer(normed, route_ids[step_at], shares, w_gate_up, w_down)
        layers.append((residual + total).astype(jnp.bfloat16))
    return (jnp.stack(attention), jnp.stack(layers))
```

```python
import math

import jax
import jax.numpy as jnp
from jax import lax
from jax.sharding import PartitionSpec as P

EPS = 1e-06
ROPE_BASE = 5000000.0


def rotate(vectors, pos_ids):
    head_size = vectors.shape[-1]
    half_dim = head_size // 2
    freq_index = jnp.arange(half_dim, dtype=jnp.int32)
    inverse_freq = jnp.exp(
        freq_index.astype(jnp.float32) * (-2.0 * math.log(ROPE_BASE) / head_size)
    )
    alternated = 60 * half_dim // 64
    axis_pick = jnp.where(freq_index < alternated, freq_index % 3, 0)
    pos_float = pos_ids.astype(jnp.float32)
    chosen = jnp.where(
        axis_pick[None, :] == 0,
        pos_float[0][:, None],
        jnp.where(axis_pick[None, :] == 1, pos_float[1][:, None], pos_float[2][:, None]),
    )
    angles = chosen * inverse_freq[None, :]
    cosine = jnp.cos(angles)[:, None, :]
    sine_part = jnp.sin(angles)[:, None, :]
    first_half = vectors[..., :half_dim]
    second_half = vectors[..., half_dim:]
    return jnp.concatenate(
        [
            first_half * cosine - second_half * sine_part,
            second_half * cosine + first_half * sine_part,
        ],
        -1,
    )


def attend(turned, cache_keys, cache_values, fresh_keys, fresh_values, lengths):
    score_scale = 1.0 / math.sqrt(turned.shape[-1])
    slot_count = cache_keys.shape[1]
    cached = (
        jnp.einsum("rhd,rld->rhl", turned, cache_keys, preferred_element_type=jnp.float32)
        * score_scale
    )
    usable = lax.broadcasted_iota(jnp.int32, (turned.shape[0], slot_count), 1) < lengths[:, None]
    cached = jnp.where(usable[:, None, :], cached, -1e30)
    recent = (
        jnp.einsum("rhd,rnd->rhn", turned, fresh_keys, preferred_element_type=jnp.float32)
        * score_scale
    )
    scores = jnp.concatenate([cached, recent], -1)
    row_max = jnp.max(scores, -1, keepdims=True)
    shifted = jnp.exp(scores - row_max)
    weights = (shifted / jnp.sum(shifted, -1, keepdims=True)).astype(jnp.bfloat16)
    mixture = jnp.einsum(
        "rhl,rld->rhd", weights[..., :slot_count], cache_values, preferred_element_type=jnp.float32
    )
    mixture = mixture + jnp.einsum(
        "rhn,rnd->rhd", weights[..., slot_count:], fresh_values, preferred_element_type=jnp.float32
    )
    return mixture.astype(jnp.bfloat16)


def per_device(
    queries,
    new_kv,
    cache,
    lengths,
    positions,
    hidden,
    norm_gain,
    route_ids,
    route_weight,
    w_gate_up,
    w_down,
):
    step_count = queries.shape[0]
    requests = queries.shape[1]
    head_dim = cache.shape[-1]
    head_count = queries.shape[2] // head_dim
    turned_keys = [
        rotate(new_kv[step_at, 0][:, None, :].astype(jnp.float32), positions[step_at])[:, 0, :]
        for step_at in range(step_count)
    ]
    fresh_keys = jnp.stack(turned_keys, 1).astype(jnp.bfloat16)
    fresh_values = jnp.transpose(new_kv[:, 1], (1, 0, 2))
    attention = []
    for step_at in range(step_count):
        turned = rotate(
            queries[step_at].reshape(requests, head_count, head_dim).astype(jnp.float32),
            positions[step_at],
        )
        turned = turned.astype(jnp.bfloat16)
        mixture = attend(
            turned,
            cache[0],
            cache[1],
            fresh_keys[:, : step_at + 1],
            fresh_values[:, : step_at + 1],
            lengths,
        )
        attention.append(mixture.reshape(requests, head_count * head_dim))
    attention = jnp.stack(attention)
    owners = lax.axis_size("dp")
    local_experts = w_down.shape[0]
    experts = owners * local_experts
    top_count = route_ids.shape[-1]
    slot_count = max(2, requests * top_count // experts)
    model_width = norm_gain.shape[0]
    hidden_part = w_down.shape[1]
    chunk = hidden.shape[-1]

    def placement_of(step_at):
        flat_ids = route_ids[step_at].reshape(-1)
        onehot = (
            flat_ids[:, None] == lax.broadcasted_iota(jnp.int32, (flat_ids.shape[0], experts), 1)
        ).astype(jnp.int32)
        rank_in = jnp.sum((jnp.cumsum(onehot, 0) - onehot) * onehot, 1)
        position = flat_ids * slot_count + rank_in
        slot_grid = lax.broadcasted_iota(jnp.int32, (experts * slot_count, requests, top_count), 0)
        placement = jnp.any(slot_grid == position.reshape(1, requests, top_count), 2).astype(
            jnp.bfloat16
        )
        return placement, position

    placements = [placement_of(step_at) for step_at in range(step_count)]
    outgoing = jnp.stack(
        [
            jnp.dot(placements[step_at][0], hidden[step_at], preferred_element_type=jnp.float32)
            .astype(jnp.bfloat16)
            .reshape(experts, slot_count, chunk)
            for step_at in range(step_count)
        ],
        1,
    ).reshape(experts, step_count * slot_count, chunk)
    received = lax.all_to_all(outgoing, "dp", split_axis=0, concat_axis=0, tiled=True)
    full_rows = lax.all_gather(received, "head", axis=2, tiled=True)
    full_rows = full_rows.reshape(-1, model_width).astype(jnp.float32)
    mean_sq = jnp.mean(full_rows * full_rows, -1, keepdims=True)
    normed = (full_rows * lax.rsqrt(mean_sq + EPS) * norm_gain).astype(jnp.bfloat16)
    gate_up = jnp.dot(normed, w_gate_up[0], preferred_element_type=jnp.float32)
    activated = (jax.nn.silu(gate_up[:, :hidden_part]) * gate_up[:, hidden_part:]).astype(
        jnp.bfloat16
    )
    partial_out = jnp.dot(activated, w_down[0], preferred_element_type=jnp.float32).astype(
        jnp.bfloat16
    )
    summed = lax.psum_scatter(partial_out, "head", scatter_dimension=1, tiled=True)
    returned = lax.all_to_all(
        summed.reshape(owners, step_count * slot_count, chunk),
        "dp",
        split_axis=0,
        concat_axis=0,
        tiled=True,
    ).reshape(experts, step_count, slot_count, chunk)

    def finish(step_at):
        table = returned[:, step_at].reshape(experts * slot_count, chunk)
        position = placements[step_at][1]
        picked = table[position].reshape(requests, top_count, chunk)
        shares = route_weight[step_at] / jnp.sum(route_weight[step_at], -1, keepdims=True)
        contrib = jnp.sum(shares[..., None] * picked.astype(jnp.float32), 1)
        return (hidden[step_at].astype(jnp.float32) + contrib).astype(jnp.bfloat16)

    layer_out = jnp.stack([finish(step_at) for step_at in range(step_count)])
    return (attention, layer_out)


def solution(mesh):
    return jax.shard_map(
        per_device,
        mesh=mesh,
        in_specs=(
            P(None, "dp", "head"),
            P(None, None, "dp", "head"),
            P(None, "dp", None, "head"),
            P("dp"),
            P(None, None, "dp"),
            P(None, "dp", "head"),
            P(),
            P(None, "dp", None),
            P(None, "dp", None),
            P("dp", None, "head"),
            P("dp", "head", None),
        ),
        out_specs=(P(None, "dp", "head"), P(None, "dp", "head")),
        check_vma=False,
    )
```

```python
import math

import jax
import jax.numpy as jnp
from jax import lax
from jax.sharding import PartitionSpec as P

EPS = 1e-06
ROPE_BASE = 5000000.0


def rotate(vectors, pos_ids):
    head_size = vectors.shape[-1]
    half_dim = head_size // 2
    freq_index = jnp.arange(half_dim, dtype=jnp.int32)
    inverse_freq = jnp.exp(
        freq_index.astype(jnp.float32) * (-2.0 * math.log(ROPE_BASE) / head_size)
    )
    alternated = 60 * half_dim // 64
    axis_pick = jnp.where(freq_index < alternated, freq_index % 3, 0)
    pos_float = pos_ids.astype(jnp.float32)
    chosen = jnp.where(
        axis_pick[None, :] == 0,
        pos_float[0][:, None],
        jnp.where(axis_pick[None, :] == 1, pos_float[1][:, None], pos_float[2][:, None]),
    )
    angles = chosen * inverse_freq[None, :]
    cosine = jnp.cos(angles)[:, None, :]
    sine_part = jnp.sin(angles)[:, None, :]
    first_half = vectors[..., :half_dim]
    second_half = vectors[..., half_dim:]
    return jnp.concatenate(
        [
            first_half * cosine - second_half * sine_part,
            second_half * cosine + first_half * sine_part,
        ],
        -1,
    )


def attend(turned, cache_keys, cache_values, fresh_keys, fresh_values, lengths):
    score_scale = 1.0 / math.sqrt(turned.shape[-1])
    slot_count = cache_keys.shape[1]
    cached = (
        jnp.einsum("rhd,rld->rhl", turned, cache_keys, preferred_element_type=jnp.float32)
        * score_scale
    )
    usable = lax.broadcasted_iota(jnp.int32, (turned.shape[0], slot_count), 1) < lengths[:, None]
    cached = jnp.where(usable[:, None, :], cached, -1e30)
    recent = (
        jnp.einsum("rhd,rnd->rhn", turned, fresh_keys, preferred_element_type=jnp.float32)
        * score_scale
    )
    scores = jnp.concatenate([cached, recent], -1)
    row_max = jnp.max(scores, -1, keepdims=True)
    shifted = jnp.exp(scores - row_max)
    weights = (shifted / jnp.sum(shifted, -1, keepdims=True)).astype(jnp.bfloat16)
    mixture = jnp.einsum(
        "rhl,rld->rhd", weights[..., :slot_count], cache_values, preferred_element_type=jnp.float32
    )
    mixture = mixture + jnp.einsum(
        "rhn,rnd->rhd", weights[..., slot_count:], fresh_values, preferred_element_type=jnp.float32
    )
    return mixture.astype(jnp.bfloat16)


def per_device(
    queries,
    new_kv,
    cache,
    lengths,
    positions,
    hidden,
    norm_gain,
    route_ids,
    route_weight,
    w_gate_up,
    w_down,
):
    step_count = queries.shape[0]
    requests = queries.shape[1]
    head_dim = cache.shape[-1]
    head_count = queries.shape[2] // head_dim
    turned_keys = [
        rotate(new_kv[step_at, 0][:, None, :].astype(jnp.float32), positions[step_at])[:, 0, :]
        for step_at in range(step_count)
    ]
    fresh_keys = jnp.stack(turned_keys, 1).astype(jnp.bfloat16)
    fresh_values = jnp.transpose(new_kv[:, 1], (1, 0, 2))
    attention = []
    for step_at in range(step_count):
        turned = rotate(
            queries[step_at].reshape(requests, head_count, head_dim).astype(jnp.float32),
            positions[step_at],
        )
        turned = turned.astype(jnp.bfloat16)
        mixture = attend(
            turned,
            cache[0],
            cache[1],
            fresh_keys[:, : step_at + 1],
            fresh_values[:, : step_at + 1],
            lengths,
        )
        attention.append(mixture.reshape(requests, head_count * head_dim))
    attention = jnp.stack(attention)
    owners = lax.axis_size("dp")
    groups = lax.axis_size("head")
    local_experts = w_down.shape[0]
    experts = owners * local_experts
    top_count = route_ids.shape[-1]
    slot_count = max(2, requests * top_count // experts)
    model_width = norm_gain.shape[0]
    hidden_part = w_down.shape[1]
    chunk = hidden.shape[-1]
    tokens = step_count * requests
    slots = step_count * slot_count

    slot_of = []
    for step_at in range(step_count):
        flat_ids = route_ids[step_at].reshape(-1)
        onehot = (
            flat_ids[:, None] == lax.broadcasted_iota(jnp.int32, (flat_ids.shape[0], experts), 1)
        ).astype(jnp.int32)
        rank_in = jnp.sum((jnp.cumsum(onehot, 0) - onehot) * onehot, 1)
        slot_of.append((flat_ids * slots + step_at * slot_count + rank_in).reshape(requests, top_count))
    slot_of = jnp.concatenate(slot_of, 0)
    slot_grid = lax.broadcasted_iota(jnp.int32, (experts, slots, tokens, top_count), 0) * slots + (
        lax.broadcasted_iota(jnp.int32, (experts, slots, tokens, top_count), 1)
    )
    hit = slot_grid == slot_of[None, None]
    placement = jnp.any(hit, 3).astype(jnp.bfloat16)
    own_rows = hidden.reshape(tokens, chunk)
    outgoing = jnp.einsum(
        "ejt,tf->ejf", placement, own_rows, preferred_element_type=jnp.float32
    ).astype(jnp.bfloat16)
    received = lax.all_to_all(outgoing, "dp", split_axis=0, concat_axis=0, tiled=True)
    gathered = lax.all_gather(received, "head", axis=0, tiled=False)
    wide = gathered.astype(jnp.float32)
    mean_sq = jnp.sum(wide * wide, (0, 3)) / model_width
    scale = lax.rsqrt(mean_sq + EPS)
    gain = norm_gain.reshape(groups, 1, 1, chunk).astype(jnp.float32)
    normed = (wide * scale[None, :, :, None] * gain).astype(jnp.bfloat16)
    gate_up = jnp.einsum(
        "hisf,hfc->isc",
        normed,
        w_gate_up[0].reshape(groups, chunk, 2 * hidden_part),
        preferred_element_type=jnp.float32,
    )
    activated = (jax.nn.silu(gate_up[..., :hidden_part]) * gate_up[..., hidden_part:]).astype(
        jnp.bfloat16
    )
    partial_out = jnp.einsum(
        "isk,khf->hisf",
        activated,
        w_down[0].reshape(hidden_part, groups, chunk),
        preferred_element_type=jnp.float32,
    ).astype(jnp.bfloat16)
    summed = lax.psum_scatter(
        partial_out.reshape(groups * experts * slots, chunk), "head", scatter_dimension=0, tiled=True
    )
    returned = lax.all_to_all(
        summed.reshape(experts, slots, chunk), "dp", split_axis=0, concat_axis=0, tiled=True
    )

    shares = route_weight / jnp.sum(route_weight, -1, keepdims=True)
    combine = jnp.sum(
        jnp.where(hit, shares.reshape(1, 1, tokens, top_count), 0.0), 3
    )
    contrib = jnp.einsum(
        "ejt,ejf->tf",
        combine,
        returned.astype(jnp.float32),
        precision=lax.Precision.HIGHEST,
        preferred_element_type=jnp.float32,
    )
    layer_out = (own_rows.astype(jnp.float32) + contrib).astype(jnp.bfloat16)
    layer_out = layer_out.reshape(step_count, requests, chunk)
    return (attention, layer_out)


def solution(mesh):
    return jax.shard_map(
        per_device,
        mesh=mesh,
        in_specs=(
            P(None, "dp", "head"),
            P(None, None, "dp", "head"),
            P(None, "dp", None, "head"),
            P("dp"),
            P(None, None, "dp"),
            P(None, "dp", "head"),
            P(),
            P(None, "dp", None),
            P(None, "dp", None),
            P("dp", None, "head"),
            P("dp", "head", None),
        ),
        out_specs=(P(None, "dp", "head"), P(None, "dp", "head")),
        check_vma=False,
    )
```

```python
import math

import jax
import jax.numpy as jnp
from jax import lax
from jax.sharding import PartitionSpec as P

EPS = 1e-06
ROPE_BASE = 5000000.0


def rotate(vectors, pos_ids):
    head_size = vectors.shape[-1]
    half_dim = head_size // 2
    freq_index = jnp.arange(half_dim, dtype=jnp.int32)
    inverse_freq = jnp.exp(
        freq_index.astype(jnp.float32) * (-2.0 * math.log(ROPE_BASE) / head_size)
    )
    alternated = 60 * half_dim // 64
    axis_pick = jnp.where(freq_index < alternated, freq_index % 3, 0)
    pos_float = pos_ids.astype(jnp.float32)
    chosen = jnp.where(
        axis_pick[None, :] == 0,
        pos_float[0][:, None],
        jnp.where(axis_pick[None, :] == 1, pos_float[1][:, None], pos_float[2][:, None]),
    )
    angles = chosen * inverse_freq[None, :]
    cosine = jnp.cos(angles)[:, None, :]
    sine_part = jnp.sin(angles)[:, None, :]
    first_half = vectors[..., :half_dim]
    second_half = vectors[..., half_dim:]
    return jnp.concatenate(
        [
            first_half * cosine - second_half * sine_part,
            second_half * cosine + first_half * sine_part,
        ],
        -1,
    )


def attend(turned, cache_keys, cache_values, fresh_keys, fresh_values, lengths):
    score_scale = 1.0 / math.sqrt(turned.shape[-1])
    slot_count = cache_keys.shape[1]
    cached = (
        jnp.einsum("rhd,rld->rhl", turned, cache_keys, preferred_element_type=jnp.float32)
        * score_scale
    )
    usable = lax.broadcasted_iota(jnp.int32, (turned.shape[0], slot_count), 1) < lengths[:, None]
    cached = jnp.where(usable[:, None, :], cached, -1e30)
    recent = (
        jnp.einsum("rhd,rnd->rhn", turned, fresh_keys, preferred_element_type=jnp.float32)
        * score_scale
    )
    scores = jnp.concatenate([cached, recent], -1)
    row_max = jnp.max(scores, -1, keepdims=True)
    shifted = jnp.exp(scores - row_max)
    weights = (shifted / jnp.sum(shifted, -1, keepdims=True)).astype(jnp.bfloat16)
    mixture = jnp.einsum(
        "rhl,rld->rhd", weights[..., :slot_count], cache_values, preferred_element_type=jnp.float32
    )
    mixture = mixture + jnp.einsum(
        "rhn,rnd->rhd", weights[..., slot_count:], fresh_values, preferred_element_type=jnp.float32
    )
    return mixture.astype(jnp.bfloat16)


def per_device(
    queries,
    new_kv,
    cache,
    lengths,
    positions,
    hidden,
    norm_gain,
    route_ids,
    route_weight,
    w_gate_up,
    w_down,
):
    step_count = queries.shape[0]
    requests = queries.shape[1]
    head_dim = cache.shape[-1]
    head_count = queries.shape[2] // head_dim
    turned_keys = [
        rotate(new_kv[step_at, 0][:, None, :].astype(jnp.float32), positions[step_at])[:, 0, :]
        for step_at in range(step_count)
    ]
    fresh_keys = jnp.stack(turned_keys, 1).astype(jnp.bfloat16)
    fresh_values = jnp.transpose(new_kv[:, 1], (1, 0, 2))
    attention = []
    for step_at in range(step_count):
        turned = rotate(
            queries[step_at].reshape(requests, head_count, head_dim).astype(jnp.float32),
            positions[step_at],
        )
        turned = turned.astype(jnp.bfloat16)
        mixture = attend(
            turned,
            cache[0],
            cache[1],
            fresh_keys[:, : step_at + 1],
            fresh_values[:, : step_at + 1],
            lengths,
        )
        attention.append(mixture.reshape(requests, head_count * head_dim))
    attention = jnp.stack(attention)
    owners = lax.axis_size("dp")
    groups = lax.axis_size("head")
    local_experts = w_down.shape[0]
    experts = owners * local_experts
    top_count = route_ids.shape[-1]
    slot_count = max(2, requests * top_count // experts)
    model_width = norm_gain.shape[0]
    hidden_part = w_down.shape[1]
    chunk = hidden.shape[-1]
    tokens = step_count * requests
    slots = step_count * slot_count

    slot_of = []
    for step_at in range(step_count):
        flat_ids = route_ids[step_at].reshape(-1)
        onehot = (
            flat_ids[:, None] == lax.broadcasted_iota(jnp.int32, (flat_ids.shape[0], experts), 1)
        ).astype(jnp.int32)
        rank_in = jnp.sum((jnp.cumsum(onehot, 0) - onehot) * onehot, 1)
        slot_of.append((flat_ids * slots + step_at * slot_count + rank_in).reshape(requests, top_count))
    slot_of = jnp.concatenate(slot_of, 0)
    slot_grid = lax.broadcasted_iota(jnp.int32, (experts, slots, tokens, top_count), 0) * slots + (
        lax.broadcasted_iota(jnp.int32, (experts, slots, tokens, top_count), 1)
    )
    hit = slot_grid == slot_of[None, None]
    placement = jnp.any(hit, 3).astype(jnp.bfloat16)
    own_rows = hidden.reshape(tokens, chunk)
    outgoing = jnp.einsum(
        "ejt,tf->ejf", placement, own_rows, preferred_element_type=jnp.float32
    ).astype(jnp.bfloat16)
    received = lax.all_to_all(outgoing, "dp", split_axis=0, concat_axis=0, tiled=True)
    received = received.reshape(experts * slots, chunk)
    gathered = lax.all_gather(received, "head", axis=0, tiled=False)
    wide = gathered.astype(jnp.float32)
    mean_sq = jnp.sum(jnp.sum(wide * wide, 2), 0) / model_width
    scale = lax.rsqrt(mean_sq + EPS)
    gain = norm_gain.reshape(groups, 1, chunk).astype(jnp.float32)
    normed = (wide * scale[None, :, None] * gain).astype(jnp.bfloat16)
    gate_up = jnp.einsum(
        "hrf,hfc->rc",
        normed,
        w_gate_up[0].reshape(groups, chunk, 2 * hidden_part),
        preferred_element_type=jnp.float32,
    )
    activated = (jax.nn.silu(gate_up[:, :hidden_part]) * gate_up[:, hidden_part:]).astype(
        jnp.bfloat16
    )
    partial_out = jnp.stack(
        [
            jnp.dot(
                activated,
                w_down[0, :, quarter * chunk : (quarter + 1) * chunk],
                preferred_element_type=jnp.float32,
            ).astype(jnp.bfloat16)
            for quarter in range(groups)
        ]
    )
    summed = lax.psum_scatter(
        partial_out.reshape(groups * experts * slots, chunk), "head", scatter_dimension=0, tiled=True
    )
    returned = lax.all_to_all(
        summed.reshape(experts, slots, chunk), "dp", split_axis=0, concat_axis=0, tiled=True
    )

    shares = route_weight / jnp.sum(route_weight, -1, keepdims=True)
    combine = jnp.sum(
        jnp.where(hit, shares.reshape(1, 1, tokens, top_count), 0.0), 3
    )
    contrib = jnp.einsum(
        "ejt,ejf->tf",
        combine,
        returned.astype(jnp.float32),
        precision=lax.Precision.HIGHEST,
        preferred_element_type=jnp.float32,
    )
    layer_out = (own_rows.astype(jnp.float32) + contrib).astype(jnp.bfloat16)
    layer_out = layer_out.reshape(step_count, requests, chunk)
    return (attention, layer_out)


def solution(mesh):
    return jax.shard_map(
        per_device,
        mesh=mesh,
        in_specs=(
            P(None, "dp", "head"),
            P(None, None, "dp", "head"),
            P(None, "dp", None, "head"),
            P("dp"),
            P(None, None, "dp"),
            P(None, "dp", "head"),
            P(),
            P(None, "dp", None),
            P(None, "dp", None),
            P("dp", None, "head"),
            P("dp", "head", None),
        ),
        out_specs=(P(None, "dp", "head"), P(None, "dp", "head")),
        check_vma=False,
    )
```

```python
import math

import jax
import jax.numpy as jnp
from jax import lax
from jax.sharding import PartitionSpec as P

EPS = 1e-06
ROPE_BASE = 5000000.0


def rotate(vectors, pos_ids):
    head_size = vectors.shape[-1]
    half_dim = head_size // 2
    freq_index = jnp.arange(half_dim, dtype=jnp.int32)
    inverse_freq = jnp.exp(
        freq_index.astype(jnp.float32) * (-2.0 * math.log(ROPE_BASE) / head_size)
    )
    alternated = 60 * half_dim // 64
    axis_pick = jnp.where(freq_index < alternated, freq_index % 3, 0)
    pos_float = pos_ids.astype(jnp.float32)
    chosen = jnp.where(
        axis_pick[None, :] == 0,
        pos_float[0][:, None],
        jnp.where(axis_pick[None, :] == 1, pos_float[1][:, None], pos_float[2][:, None]),
    )
    angles = chosen * inverse_freq[None, :]
    cosine = jnp.cos(angles)[:, None, :]
    sine_part = jnp.sin(angles)[:, None, :]
    first_half = vectors[..., :half_dim]
    second_half = vectors[..., half_dim:]
    return jnp.concatenate(
        [
            first_half * cosine - second_half * sine_part,
            second_half * cosine + first_half * sine_part,
        ],
        -1,
    )


def attend(turned, cache_keys, cache_values, fresh_keys, fresh_values, lengths):
    score_scale = 1.0 / math.sqrt(turned.shape[-1])
    slot_count = cache_keys.shape[1]
    cached = (
        jnp.einsum("rhd,rld->rhl", turned, cache_keys, preferred_element_type=jnp.float32)
        * score_scale
    )
    usable = lax.broadcasted_iota(jnp.int32, (turned.shape[0], slot_count), 1) < lengths[:, None]
    cached = jnp.where(usable[:, None, :], cached, -1e30)
    recent = (
        jnp.einsum("rhd,rnd->rhn", turned, fresh_keys, preferred_element_type=jnp.float32)
        * score_scale
    )
    scores = jnp.concatenate([cached, recent], -1)
    row_max = jnp.max(scores, -1, keepdims=True)
    shifted = jnp.exp(scores - row_max)
    weights = (shifted / jnp.sum(shifted, -1, keepdims=True)).astype(jnp.bfloat16)
    mixture = jnp.einsum(
        "rhl,rld->rhd", weights[..., :slot_count], cache_values, preferred_element_type=jnp.float32
    )
    mixture = mixture + jnp.einsum(
        "rhn,rnd->rhd", weights[..., slot_count:], fresh_values, preferred_element_type=jnp.float32
    )
    return mixture.astype(jnp.bfloat16)


def per_device(
    queries,
    new_kv,
    cache,
    lengths,
    positions,
    hidden,
    norm_gain,
    route_ids,
    route_weight,
    w_gate_up,
    w_down,
):
    step_count = queries.shape[0]
    requests = queries.shape[1]
    head_dim = cache.shape[-1]
    head_count = queries.shape[2] // head_dim
    turned_keys = [
        rotate(new_kv[step_at, 0][:, None, :].astype(jnp.float32), positions[step_at])[:, 0, :]
        for step_at in range(step_count)
    ]
    fresh_keys = jnp.stack(turned_keys, 1).astype(jnp.bfloat16)
    fresh_values = jnp.transpose(new_kv[:, 1], (1, 0, 2))
    attention = []
    for step_at in range(step_count):
        turned = rotate(
            queries[step_at].reshape(requests, head_count, head_dim).astype(jnp.float32),
            positions[step_at],
        )
        turned = turned.astype(jnp.bfloat16)
        mixture = attend(
            turned,
            cache[0],
            cache[1],
            fresh_keys[:, : step_at + 1],
            fresh_values[:, : step_at + 1],
            lengths,
        )
        attention.append(mixture.reshape(requests, head_count * head_dim))
    attention = jnp.stack(attention)
    owners = lax.axis_size("dp")
    groups = lax.axis_size("head")
    local_experts = w_down.shape[0]
    experts = owners * local_experts
    top_count = route_ids.shape[-1]
    slot_count = max(2, requests * top_count // experts)
    model_width = norm_gain.shape[0]
    hidden_part = w_down.shape[1]
    chunk = hidden.shape[-1]
    tokens = step_count * requests
    slots = step_count * slot_count

    slot_of = []
    for step_at in range(step_count):
        flat_ids = route_ids[step_at].reshape(-1)
        onehot = (
            flat_ids[:, None] == lax.broadcasted_iota(jnp.int32, (flat_ids.shape[0], experts), 1)
        ).astype(jnp.int32)
        rank_in = jnp.sum((jnp.cumsum(onehot, 0) - onehot) * onehot, 1)
        slot_of.append((flat_ids * slots + step_at * slot_count + rank_in).reshape(requests, top_count))
    slot_of = jnp.concatenate(slot_of, 0)
    slot_grid = lax.broadcasted_iota(jnp.int32, (experts, slots, tokens, top_count), 0) * slots + (
        lax.broadcasted_iota(jnp.int32, (experts, slots, tokens, top_count), 1)
    )
    hit = slot_grid == slot_of[None, None]
    placement = jnp.any(hit, 3).astype(jnp.bfloat16)
    own_rows = hidden.reshape(tokens, chunk)
    outgoing = jnp.einsum(
        "ejt,tf->ejf", placement, own_rows, preferred_element_type=jnp.float32
    ).astype(jnp.bfloat16)
    received = lax.all_to_all(outgoing, "dp", split_axis=0, concat_axis=0, tiled=True)
    received = received.reshape(experts * slots, chunk)
    gathered = lax.all_to_all(
        jnp.broadcast_to(received[None], (groups,) + received.shape),
        "head",
        split_axis=0,
        concat_axis=0,
        tiled=True,
    )
    wide = gathered.astype(jnp.float32)
    mean_sq = jnp.sum(jnp.sum(wide * wide, 2), 0) / model_width
    scale = lax.rsqrt(mean_sq + EPS)
    gain = norm_gain.reshape(groups, 1, chunk).astype(jnp.float32)
    normed = (wide * scale[None, :, None] * gain).astype(jnp.bfloat16)
    gate_up = jnp.einsum(
        "hrf,hfc->rc",
        normed,
        w_gate_up[0].reshape(groups, chunk, 2 * hidden_part),
        preferred_element_type=jnp.float32,
    )
    activated = (jax.nn.silu(gate_up[:, :hidden_part]) * gate_up[:, hidden_part:]).astype(
        jnp.bfloat16
    )
    partial_out = jnp.stack(
        [
            jnp.dot(
                activated,
                w_down[0, :, quarter * chunk : (quarter + 1) * chunk],
                preferred_element_type=jnp.float32,
            ).astype(jnp.bfloat16)
            for quarter in range(groups)
        ]
    )
    summed = jnp.sum(
        lax.all_to_all(partial_out, "head", split_axis=0, concat_axis=0, tiled=True).astype(
            jnp.float32
        ),
        0,
    ).astype(jnp.bfloat16)
    returned = lax.all_to_all(
        summed.reshape(experts, slots, chunk), "dp", split_axis=0, concat_axis=0, tiled=True
    )

    shares = route_weight / jnp.sum(route_weight, -1, keepdims=True)
    combine = jnp.sum(
        jnp.where(hit, shares.reshape(1, 1, tokens, top_count), 0.0), 3
    )
    contrib = jnp.einsum(
        "ejt,ejf->tf",
        combine,
        returned.astype(jnp.float32),
        precision=lax.Precision.HIGHEST,
        preferred_element_type=jnp.float32,
    )
    layer_out = (own_rows.astype(jnp.float32) + contrib).astype(jnp.bfloat16)
    layer_out = layer_out.reshape(step_count, requests, chunk)
    return (attention, layer_out)


def solution(mesh):
    return jax.shard_map(
        per_device,
        mesh=mesh,
        in_specs=(
            P(None, "dp", "head"),
            P(None, None, "dp", "head"),
            P(None, "dp", None, "head"),
            P("dp"),
            P(None, None, "dp"),
            P(None, "dp", "head"),
            P(),
            P(None, "dp", None),
            P(None, "dp", None),
            P("dp", None, "head"),
            P("dp", "head", None),
        ),
        out_specs=(P(None, "dp", "head"), P(None, "dp", "head")),
        check_vma=False,
    )
```

```python
import math

import jax
import jax.numpy as jnp
from jax import lax
from jax.sharding import PartitionSpec as P

EPS = 1e-06
ROPE_BASE = 5000000.0


def rotate(vectors, pos_ids):
    head_size = vectors.shape[-1]
    half_dim = head_size // 2
    freq_index = jnp.arange(half_dim, dtype=jnp.int32)
    inverse_freq = jnp.exp(
        freq_index.astype(jnp.float32) * (-2.0 * math.log(ROPE_BASE) / head_size)
    )
    alternated = 60 * half_dim // 64
    axis_pick = jnp.where(freq_index < alternated, freq_index % 3, 0)
    pos_float = pos_ids.astype(jnp.float32)
    chosen = jnp.where(
        axis_pick[None, :] == 0,
        pos_float[0][:, None],
        jnp.where(axis_pick[None, :] == 1, pos_float[1][:, None], pos_float[2][:, None]),
    )
    angles = chosen * inverse_freq[None, :]
    cosine = jnp.cos(angles)[:, None, :]
    sine_part = jnp.sin(angles)[:, None, :]
    first_half = vectors[..., :half_dim]
    second_half = vectors[..., half_dim:]
    return jnp.concatenate(
        [
            first_half * cosine - second_half * sine_part,
            second_half * cosine + first_half * sine_part,
        ],
        -1,
    )


def attend(turned, cache_keys, cache_values, fresh_keys, fresh_values, lengths):
    score_scale = 1.0 / math.sqrt(turned.shape[-1])
    slot_count = cache_keys.shape[1]
    cached = (
        jnp.einsum("rhd,rld->rhl", turned, cache_keys, preferred_element_type=jnp.float32)
        * score_scale
    )
    usable = lax.broadcasted_iota(jnp.int32, (turned.shape[0], slot_count), 1) < lengths[:, None]
    cached = jnp.where(usable[:, None, :], cached, -1e30)
    recent = (
        jnp.einsum("rhd,rnd->rhn", turned, fresh_keys, preferred_element_type=jnp.float32)
        * score_scale
    )
    scores = jnp.concatenate([cached, recent], -1)
    row_max = jnp.max(scores, -1, keepdims=True)
    shifted = jnp.exp(scores - row_max)
    weights = (shifted / jnp.sum(shifted, -1, keepdims=True)).astype(jnp.bfloat16)
    mixture = jnp.einsum(
        "rhl,rld->rhd", weights[..., :slot_count], cache_values, preferred_element_type=jnp.float32
    )
    mixture = mixture + jnp.einsum(
        "rhn,rnd->rhd", weights[..., slot_count:], fresh_values, preferred_element_type=jnp.float32
    )
    return mixture.astype(jnp.bfloat16)


def per_device(
    queries,
    new_kv,
    cache,
    lengths,
    positions,
    hidden,
    norm_gain,
    route_ids,
    route_weight,
    w_gate_up,
    w_down,
):
    step_count = queries.shape[0]
    requests = queries.shape[1]
    head_dim = cache.shape[-1]
    head_count = queries.shape[2] // head_dim
    turned_keys = [
        rotate(new_kv[step_at, 0][:, None, :].astype(jnp.float32), positions[step_at])[:, 0, :]
        for step_at in range(step_count)
    ]
    fresh_keys = jnp.stack(turned_keys, 1).astype(jnp.bfloat16)
    fresh_values = jnp.transpose(new_kv[:, 1], (1, 0, 2))
    attention = []
    for step_at in range(step_count):
        turned = rotate(
            queries[step_at].reshape(requests, head_count, head_dim).astype(jnp.float32),
            positions[step_at],
        )
        turned = turned.astype(jnp.bfloat16)
        mixture = attend(
            turned,
            cache[0],
            cache[1],
            fresh_keys[:, : step_at + 1],
            fresh_values[:, : step_at + 1],
            lengths,
        )
        attention.append(mixture.reshape(requests, head_count * head_dim))
    attention = jnp.stack(attention)
    owners = lax.axis_size("dp")
    groups = lax.axis_size("head")
    local_experts = w_down.shape[0]
    experts = owners * local_experts
    top_count = route_ids.shape[-1]
    slot_count = max(2, requests * top_count // experts)
    model_width = norm_gain.shape[0]
    hidden_part = w_down.shape[1]
    chunk = hidden.shape[-1]
    tokens = step_count * requests
    slots = step_count * slot_count

    slot_of = []
    for step_at in range(step_count):
        flat_ids = route_ids[step_at].reshape(-1)
        onehot = (
            flat_ids[:, None] == lax.broadcasted_iota(jnp.int32, (flat_ids.shape[0], experts), 1)
        ).astype(jnp.int32)
        rank_in = jnp.sum((jnp.cumsum(onehot, 0) - onehot) * onehot, 1)
        slot_of.append((flat_ids * slots + step_at * slot_count + rank_in).reshape(requests, top_count))
    slot_of = jnp.concatenate(slot_of, 0)
    slot_grid = lax.broadcasted_iota(jnp.int32, (experts, slots, tokens, top_count), 0) * slots + (
        lax.broadcasted_iota(jnp.int32, (experts, slots, tokens, top_count), 1)
    )
    hit = slot_grid == slot_of[None, None]
    placement = jnp.any(hit, 3).astype(jnp.bfloat16)
    own_rows = hidden.reshape(tokens, chunk)
    outgoing = jnp.einsum(
        "ejt,tf->ejf", placement, own_rows, preferred_element_type=jnp.float32
    ).astype(jnp.bfloat16)
    received = lax.all_to_all(outgoing, "dp", split_axis=0, concat_axis=0, tiled=True)
    received = received.reshape(experts * slots, chunk)
    assert groups == 4
    me = lax.axis_index("head")
    to_right = [(j, (j + 1) % groups) for j in range(groups)]
    to_left = [(j, (j - 1) % groups) for j in range(groups)]
    half = received.shape[0] // 2
    from_left = lax.ppermute(received, "head", to_right)
    from_right = lax.ppermute(received, "head", to_left)
    far = jnp.concatenate(
        [
            lax.ppermute(from_left[:half], "head", to_right),
            lax.ppermute(from_right[half:], "head", to_left),
        ],
        0,
    )
    gathered = jnp.stack([received, from_right, far, from_left])
    quarter_at = [(me + k) % groups for k in range(groups)]
    wide = gathered.astype(jnp.float32)
    mean_sq = jnp.sum(jnp.sum(wide * wide, 2), 0) / model_width
    scale = lax.rsqrt(mean_sq + EPS)
    gain = jnp.stack(
        [lax.dynamic_slice_in_dim(norm_gain, q * chunk, chunk) for q in quarter_at]
    ).astype(jnp.float32)
    normed = (wide * scale[None, :, None] * gain[:, None, :]).astype(jnp.bfloat16)
    up_rows = jnp.stack(
        [lax.dynamic_slice_in_dim(w_gate_up[0], q * chunk, chunk, 0) for q in quarter_at]
    )
    gate_up = jnp.einsum("hrf,hfc->rc", normed, up_rows, preferred_element_type=jnp.float32)
    activated = (jax.nn.silu(gate_up[:, :hidden_part]) * gate_up[:, hidden_part:]).astype(
        jnp.bfloat16
    )
    partial_out = [
        jnp.dot(
            activated,
            lax.dynamic_slice_in_dim(w_down[0], q * chunk, chunk, 1),
            preferred_element_type=jnp.float32,
        ).astype(jnp.bfloat16)
        for q in quarter_at
    ]

    def plus(a, b):
        return (a.astype(jnp.float32) + b.astype(jnp.float32)).astype(jnp.bfloat16)

    far_a = lax.ppermute(partial_out[2][:half], "head", to_right)
    far_b = lax.ppermute(partial_out[2][half:], "head", to_left)
    near_r = lax.ppermute(
        jnp.concatenate([plus(partial_out[1][:half], far_a), partial_out[1][half:]], 0),
        "head",
        to_right,
    )
    near_l = lax.ppermute(
        jnp.concatenate([partial_out[3][:half], plus(partial_out[3][half:], far_b)], 0),
        "head",
        to_left,
    )
    summed = (
        partial_out[0].astype(jnp.float32) + near_r.astype(jnp.float32) + near_l.astype(jnp.float32)
    ).astype(jnp.bfloat16)
    returned = lax.all_to_all(
        summed.reshape(experts, slots, chunk), "dp", split_axis=0, concat_axis=0, tiled=True
    )

    shares = route_weight / jnp.sum(route_weight, -1, keepdims=True)
    combine = jnp.sum(
        jnp.where(hit, shares.reshape(1, 1, tokens, top_count), 0.0), 3
    )
    contrib = jnp.einsum(
        "ejt,ejf->tf",
        combine,
        returned.astype(jnp.float32),
        precision=lax.Precision.HIGHEST,
        preferred_element_type=jnp.float32,
    )
    layer_out = (own_rows.astype(jnp.float32) + contrib).astype(jnp.bfloat16)
    layer_out = layer_out.reshape(step_count, requests, chunk)
    return (attention, layer_out)


def solution(mesh):
    return jax.shard_map(
        per_device,
        mesh=mesh,
        in_specs=(
            P(None, "dp", "head"),
            P(None, None, "dp", "head"),
            P(None, "dp", None, "head"),
            P("dp"),
            P(None, None, "dp"),
            P(None, "dp", "head"),
            P(),
            P(None, "dp", None),
            P(None, "dp", None),
            P("dp", None, "head"),
            P("dp", "head", None),
        ),
        out_specs=(P(None, "dp", "head"), P(None, "dp", "head")),
        check_vma=False,
    )
```

```python
import math

import jax
import jax.numpy as jnp
from jax import lax
from jax.sharding import PartitionSpec as P

EPS = 1e-06
ROPE_BASE = 5000000.0


def rotate(vectors, pos_ids):
    head_size = vectors.shape[-1]
    half_dim = head_size // 2
    freq_index = jnp.arange(half_dim, dtype=jnp.int32)
    inverse_freq = jnp.exp(
        freq_index.astype(jnp.float32) * (-2.0 * math.log(ROPE_BASE) / head_size)
    )
    alternated = 60 * half_dim // 64
    axis_pick = jnp.where(freq_index < alternated, freq_index % 3, 0)
    pos_float = pos_ids.astype(jnp.float32)
    chosen = jnp.where(
        axis_pick[None, :] == 0,
        pos_float[0][:, None],
        jnp.where(axis_pick[None, :] == 1, pos_float[1][:, None], pos_float[2][:, None]),
    )
    angles = chosen * inverse_freq[None, :]
    cosine = jnp.cos(angles)[:, None, :]
    sine_part = jnp.sin(angles)[:, None, :]
    first_half = vectors[..., :half_dim]
    second_half = vectors[..., half_dim:]
    return jnp.concatenate(
        [
            first_half * cosine - second_half * sine_part,
            second_half * cosine + first_half * sine_part,
        ],
        -1,
    )


def attend(turned, cache_keys, cache_values, fresh_keys, fresh_values, lengths):
    score_scale = 1.0 / math.sqrt(turned.shape[-1])
    slot_count = cache_keys.shape[1]
    cached = (
        jnp.einsum("rhd,rld->rhl", turned, cache_keys, preferred_element_type=jnp.float32)
        * score_scale
    )
    usable = lax.broadcasted_iota(jnp.int32, (turned.shape[0], slot_count), 1) < lengths[:, None]
    cached = jnp.where(usable[:, None, :], cached, -1e30)
    recent = (
        jnp.einsum("rhd,rnd->rhn", turned, fresh_keys, preferred_element_type=jnp.float32)
        * score_scale
    )
    scores = jnp.concatenate([cached, recent], -1)
    row_max = jnp.max(scores, -1, keepdims=True)
    shifted = jnp.exp(scores - row_max)
    weights = (shifted / jnp.sum(shifted, -1, keepdims=True)).astype(jnp.bfloat16)
    mixture = jnp.einsum(
        "rhl,rld->rhd", weights[..., :slot_count], cache_values, preferred_element_type=jnp.float32
    )
    mixture = mixture + jnp.einsum(
        "rhn,rnd->rhd", weights[..., slot_count:], fresh_values, preferred_element_type=jnp.float32
    )
    return mixture.astype(jnp.bfloat16)


def per_device(
    queries,
    new_kv,
    cache,
    lengths,
    positions,
    hidden,
    norm_gain,
    route_ids,
    route_weight,
    w_gate_up,
    w_down,
):
    step_count = queries.shape[0]
    requests = queries.shape[1]
    head_dim = cache.shape[-1]
    head_count = queries.shape[2] // head_dim
    turned_keys = [
        rotate(new_kv[step_at, 0][:, None, :].astype(jnp.float32), positions[step_at])[:, 0, :]
        for step_at in range(step_count)
    ]
    fresh_keys = jnp.stack(turned_keys, 1).astype(jnp.bfloat16)
    fresh_values = jnp.transpose(new_kv[:, 1], (1, 0, 2))
    attention = []
    for step_at in range(step_count):
        turned = rotate(
            queries[step_at].reshape(requests, head_count, head_dim).astype(jnp.float32),
            positions[step_at],
        )
        turned = turned.astype(jnp.bfloat16)
        mixture = attend(
            turned,
            cache[0],
            cache[1],
            fresh_keys[:, : step_at + 1],
            fresh_values[:, : step_at + 1],
            lengths,
        )
        attention.append(mixture.reshape(requests, head_count * head_dim))
    attention = jnp.stack(attention)
    owners = lax.axis_size("dp")
    groups = lax.axis_size("head")
    local_experts = w_down.shape[0]
    experts = owners * local_experts
    top_count = route_ids.shape[-1]
    slot_count = max(2, requests * top_count // experts)
    model_width = norm_gain.shape[0]
    hidden_part = w_down.shape[1]
    chunk = hidden.shape[-1]
    tokens = step_count * requests
    slots = step_count * slot_count

    slot_of = []
    for step_at in range(step_count):
        flat_ids = route_ids[step_at].reshape(-1)
        onehot = (
            flat_ids[:, None] == lax.broadcasted_iota(jnp.int32, (flat_ids.shape[0], experts), 1)
        ).astype(jnp.int32)
        rank_in = jnp.sum((jnp.cumsum(onehot, 0) - onehot) * onehot, 1)
        slot_of.append((flat_ids * slots + step_at * slot_count + rank_in).reshape(requests, top_count))
    slot_of = jnp.concatenate(slot_of, 0)
    slot_grid = lax.broadcasted_iota(jnp.int32, (experts, slots, tokens, top_count), 0) * slots + (
        lax.broadcasted_iota(jnp.int32, (experts, slots, tokens, top_count), 1)
    )
    hit = slot_grid == slot_of[None, None]
    placement = jnp.any(hit, 3).astype(jnp.bfloat16)
    own_rows = hidden.reshape(tokens, chunk)
    outgoing = jnp.einsum(
        "ejt,tf->ejf", placement, own_rows, preferred_element_type=jnp.float32
    ).astype(jnp.bfloat16)
    received = lax.all_to_all(outgoing, "dp", split_axis=0, concat_axis=0, tiled=True)
    received = received.reshape(experts * slots, chunk)
    assert groups == 4
    me = lax.axis_index("head")
    to_right = [(j, (j + 1) % groups) for j in range(groups)]
    to_left = [(j, (j - 1) % groups) for j in range(groups)]
    half = received.shape[0] // 2
    from_left = lax.ppermute(received, "head", to_right)
    from_right = lax.ppermute(received, "head", to_left)
    far = jnp.concatenate(
        [
            lax.ppermute(from_left[:half], "head", to_right),
            lax.ppermute(from_right[half:], "head", to_left),
        ],
        0,
    )
    blocks = [received, from_right, far, from_left]
    quarter_at = [(me + k) % groups for k in range(groups)]
    wide = [block.astype(jnp.float32) for block in blocks]
    mean_sq = sum(jnp.sum(block * block, 1) for block in wide) / model_width
    scale = lax.rsqrt(mean_sq + EPS)[:, None]
    gate_up = None
    for block, q in zip(wide, quarter_at):
        gain = lax.dynamic_slice_in_dim(norm_gain, q * chunk, chunk).astype(jnp.float32)
        normed = (block * scale * gain[None, :]).astype(jnp.bfloat16)
        term = jnp.dot(
            normed,
            lax.dynamic_slice_in_dim(w_gate_up[0], q * chunk, chunk, 0),
            preferred_element_type=jnp.float32,
        )
        gate_up = term if gate_up is None else gate_up + term
    activated = (jax.nn.silu(gate_up[:, :hidden_part]) * gate_up[:, hidden_part:]).astype(
        jnp.bfloat16
    )
    partial_out = [
        jnp.dot(
            activated,
            lax.dynamic_slice_in_dim(w_down[0], q * chunk, chunk, 1),
            preferred_element_type=jnp.float32,
        ).astype(jnp.bfloat16)
        for q in quarter_at
    ]

    def plus(a, b):
        return (a.astype(jnp.float32) + b.astype(jnp.float32)).astype(jnp.bfloat16)

    far_a = lax.ppermute(partial_out[2][:half], "head", to_right)
    far_b = lax.ppermute(partial_out[2][half:], "head", to_left)
    near_r = lax.ppermute(
        jnp.concatenate([plus(partial_out[1][:half], far_a), partial_out[1][half:]], 0),
        "head",
        to_right,
    )
    near_l = lax.ppermute(
        jnp.concatenate([partial_out[3][:half], plus(partial_out[3][half:], far_b)], 0),
        "head",
        to_left,
    )
    summed = (
        partial_out[0].astype(jnp.float32) + near_r.astype(jnp.float32) + near_l.astype(jnp.float32)
    ).astype(jnp.bfloat16)
    returned = lax.all_to_all(
        summed.reshape(experts, slots, chunk), "dp", split_axis=0, concat_axis=0, tiled=True
    )

    shares = route_weight / jnp.sum(route_weight, -1, keepdims=True)
    combine = jnp.sum(
        jnp.where(hit, shares.reshape(1, 1, tokens, top_count), 0.0), 3
    )
    contrib = jnp.einsum(
        "ejt,ejf->tf",
        combine,
        returned.astype(jnp.float32),
        precision=lax.Precision.HIGHEST,
        preferred_element_type=jnp.float32,
    )
    layer_out = (own_rows.astype(jnp.float32) + contrib).astype(jnp.bfloat16)
    layer_out = layer_out.reshape(step_count, requests, chunk)
    return (attention, layer_out)


def solution(mesh):
    return jax.shard_map(
        per_device,
        mesh=mesh,
        in_specs=(
            P(None, "dp", "head"),
            P(None, None, "dp", "head"),
            P(None, "dp", None, "head"),
            P("dp"),
            P(None, None, "dp"),
            P(None, "dp", "head"),
            P(),
            P(None, "dp", None),
            P(None, "dp", None),
            P("dp", None, "head"),
            P("dp", "head", None),
        ),
        out_specs=(P(None, "dp", "head"), P(None, "dp", "head")),
        check_vma=False,
    )
```

```python
import math

import jax
import jax.numpy as jnp
from jax import lax
from jax.sharding import PartitionSpec as P

EPS = 1e-06
ROPE_BASE = 5000000.0


def rotate(vectors, pos_ids):
    head_size = vectors.shape[-1]
    half_dim = head_size // 2
    freq_index = jnp.arange(half_dim, dtype=jnp.int32)
    inverse_freq = jnp.exp(
        freq_index.astype(jnp.float32) * (-2.0 * math.log(ROPE_BASE) / head_size)
    )
    alternated = 60 * half_dim // 64
    axis_pick = jnp.where(freq_index < alternated, freq_index % 3, 0)
    pos_float = pos_ids.astype(jnp.float32)
    chosen = jnp.where(
        axis_pick[None, :] == 0,
        pos_float[0][:, None],
        jnp.where(axis_pick[None, :] == 1, pos_float[1][:, None], pos_float[2][:, None]),
    )
    angles = chosen * inverse_freq[None, :]
    cosine = jnp.cos(angles)[:, None, :]
    sine_part = jnp.sin(angles)[:, None, :]
    first_half = vectors[..., :half_dim]
    second_half = vectors[..., half_dim:]
    return jnp.concatenate(
        [
            first_half * cosine - second_half * sine_part,
            second_half * cosine + first_half * sine_part,
        ],
        -1,
    )


def attend(turned, cache_keys, cache_values, fresh_keys, fresh_values, lengths):
    score_scale = 1.0 / math.sqrt(turned.shape[-1])
    slot_count = cache_keys.shape[1]
    cached = (
        jnp.einsum("rhd,rld->rhl", turned, cache_keys, preferred_element_type=jnp.float32)
        * score_scale
    )
    usable = lax.broadcasted_iota(jnp.int32, (turned.shape[0], slot_count), 1) < lengths[:, None]
    cached = jnp.where(usable[:, None, :], cached, -1e30)
    recent = (
        jnp.einsum("rhd,rnd->rhn", turned, fresh_keys, preferred_element_type=jnp.float32)
        * score_scale
    )
    scores = jnp.concatenate([cached, recent], -1)
    row_max = jnp.max(scores, -1, keepdims=True)
    shifted = jnp.exp(scores - row_max)
    weights = (shifted / jnp.sum(shifted, -1, keepdims=True)).astype(jnp.bfloat16)
    mixture = jnp.einsum(
        "rhl,rld->rhd", weights[..., :slot_count], cache_values, preferred_element_type=jnp.float32
    )
    mixture = mixture + jnp.einsum(
        "rhn,rnd->rhd", weights[..., slot_count:], fresh_values, preferred_element_type=jnp.float32
    )
    return mixture.astype(jnp.bfloat16)


def per_device(
    queries,
    new_kv,
    cache,
    lengths,
    positions,
    hidden,
    norm_gain,
    route_ids,
    route_weight,
    w_gate_up,
    w_down,
):
    step_count = queries.shape[0]
    requests = queries.shape[1]
    head_dim = cache.shape[-1]
    head_count = queries.shape[2] // head_dim
    turned_keys = [
        rotate(new_kv[step_at, 0][:, None, :].astype(jnp.float32), positions[step_at])[:, 0, :]
        for step_at in range(step_count)
    ]
    fresh_keys = jnp.stack(turned_keys, 1).astype(jnp.bfloat16)
    fresh_values = jnp.transpose(new_kv[:, 1], (1, 0, 2))
    attention = []
    for step_at in range(step_count):
        turned = rotate(
            queries[step_at].reshape(requests, head_count, head_dim).astype(jnp.float32),
            positions[step_at],
        )
        turned = turned.astype(jnp.bfloat16)
        mixture = attend(
            turned,
            cache[0],
            cache[1],
            fresh_keys[:, : step_at + 1],
            fresh_values[:, : step_at + 1],
            lengths,
        )
        attention.append(mixture.reshape(requests, head_count * head_dim))
    attention = jnp.stack(attention)
    owners = lax.axis_size("dp")
    groups = lax.axis_size("head")
    local_experts = w_down.shape[0]
    experts = owners * local_experts
    top_count = route_ids.shape[-1]
    slot_count = max(2, requests * top_count // experts)
    model_width = norm_gain.shape[0]
    hidden_part = w_down.shape[1]
    chunk = hidden.shape[-1]
    tokens = step_count * requests
    slots = step_count * slot_count

    slot_of = []
    for step_at in range(step_count):
        flat_ids = route_ids[step_at].reshape(-1)
        onehot = (
            flat_ids[:, None] == lax.broadcasted_iota(jnp.int32, (flat_ids.shape[0], experts), 1)
        ).astype(jnp.int32)
        rank_in = jnp.sum((jnp.cumsum(onehot, 0) - onehot) * onehot, 1)
        slot_of.append((flat_ids * slots + step_at * slot_count + rank_in).reshape(requests, top_count))
    slot_of = jnp.concatenate(slot_of, 0)
    slot_grid = lax.broadcasted_iota(jnp.int32, (experts, slots, tokens, top_count), 0) * slots + (
        lax.broadcasted_iota(jnp.int32, (experts, slots, tokens, top_count), 1)
    )
    hit = slot_grid == slot_of[None, None]
    placement = jnp.any(hit, 3).astype(jnp.bfloat16)
    own_rows = hidden.reshape(tokens, chunk)
    outgoing = jnp.einsum(
        "ejt,tf->ejf", placement, own_rows, preferred_element_type=jnp.float32
    ).astype(jnp.bfloat16)
    received = lax.all_to_all(outgoing, "dp", split_axis=0, concat_axis=0, tiled=True)
    received = received.reshape(experts * slots, chunk)
    assert groups == 4
    me = lax.axis_index("head")
    to_right = [(j, (j + 1) % groups) for j in range(groups)]
    to_left = [(j, (j - 1) % groups) for j in range(groups)]
    half = received.shape[0] // 2

    def ring_sum(terms, plus):
        far_a = lax.ppermute(terms[2][:half], "head", to_right)
        far_b = lax.ppermute(terms[2][half:], "head", to_left)
        near_r = lax.ppermute(
            jnp.concatenate([plus(terms[1][:half], far_a), terms[1][half:]], 0), "head", to_right
        )
        near_l = lax.ppermute(
            jnp.concatenate([terms[3][:half], plus(terms[3][half:], far_b)], 0), "head", to_left
        )
        return plus(plus(terms[0], near_r), near_l)

    up_cols = w_gate_up[0]
    up_blocks = [lax.dynamic_slice_in_dim(up_cols, me * chunk, chunk, 0)]
    for k in range(1, groups):
        piece = lax.dynamic_slice_in_dim(up_cols, ((me - k) % groups) * chunk, chunk, 0)
        up_blocks.append(lax.ppermute(piece, "head", [(j, (j - k) % groups) for j in range(groups)]))
    own_gain = lax.dynamic_slice_in_dim(norm_gain, me * chunk, chunk).astype(jnp.float32)
    wide = received.astype(jnp.float32)
    mean_sq = lax.psum(jnp.sum(wide * wide, 1), "head") / model_width
    scaled = (wide * own_gain[None, :]).astype(jnp.bfloat16)
    shares_of_up = jnp.einsum(
        "rf,kfc->krc", scaled, jnp.stack(up_blocks), preferred_element_type=jnp.float32
    )
    gate_up = ring_sum([shares_of_up[k] for k in range(groups)], lambda a, b: a + b)
    gate_up = gate_up * lax.rsqrt(mean_sq + EPS)[:, None]
    activated = (jax.nn.silu(gate_up[:, :hidden_part]) * gate_up[:, hidden_part:]).astype(
        jnp.bfloat16
    )
    quarter_at = [(me + k) % groups for k in range(groups)]
    partial_out = [
        jnp.dot(
            activated,
            lax.dynamic_slice_in_dim(w_down[0], q * chunk, chunk, 1),
            preferred_element_type=jnp.float32,
        ).astype(jnp.bfloat16)
        for q in quarter_at
    ]

    def plus(a, b):
        return (a.astype(jnp.float32) + b.astype(jnp.float32)).astype(jnp.bfloat16)

    summed = ring_sum(partial_out, plus)
    returned = lax.all_to_all(
        summed.reshape(experts, slots, chunk), "dp", split_axis=0, concat_axis=0, tiled=True
    )

    shares = route_weight / jnp.sum(route_weight, -1, keepdims=True)
    combine = jnp.sum(
        jnp.where(hit, shares.reshape(1, 1, tokens, top_count), 0.0), 3
    )
    contrib = jnp.einsum(
        "ejt,ejf->tf",
        combine,
        returned.astype(jnp.float32),
        precision=lax.Precision.HIGHEST,
        preferred_element_type=jnp.float32,
    )
    layer_out = (own_rows.astype(jnp.float32) + contrib).astype(jnp.bfloat16)
    layer_out = layer_out.reshape(step_count, requests, chunk)
    return (attention, layer_out)


def solution(mesh):
    return jax.shard_map(
        per_device,
        mesh=mesh,
        in_specs=(
            P(None, "dp", "head"),
            P(None, None, "dp", "head"),
            P(None, "dp", None, "head"),
            P("dp"),
            P(None, None, "dp"),
            P(None, "dp", "head"),
            P(),
            P(None, "dp", None),
            P(None, "dp", None),
            P("dp", None, "head"),
            P("dp", "head", None),
        ),
        out_specs=(P(None, "dp", "head"), P(None, "dp", "head")),
        check_vma=False,
    )
```

```python
import math

import jax
import jax.numpy as jnp
from jax import lax
from jax.sharding import PartitionSpec as P

EPS = 1e-06
ROPE_BASE = 5000000.0


def rotate(vectors, pos_ids):
    head_size = vectors.shape[-1]
    half_dim = head_size // 2
    freq_index = jnp.arange(half_dim, dtype=jnp.int32)
    inverse_freq = jnp.exp(
        freq_index.astype(jnp.float32) * (-2.0 * math.log(ROPE_BASE) / head_size)
    )
    alternated = 60 * half_dim // 64
    axis_pick = jnp.where(freq_index < alternated, freq_index % 3, 0)
    pos_float = pos_ids.astype(jnp.float32)
    chosen = jnp.where(
        axis_pick[None, :] == 0,
        pos_float[0][:, None],
        jnp.where(axis_pick[None, :] == 1, pos_float[1][:, None], pos_float[2][:, None]),
    )
    angles = chosen * inverse_freq[None, :]
    cosine = jnp.cos(angles)[:, None, :]
    sine_part = jnp.sin(angles)[:, None, :]
    first_half = vectors[..., :half_dim]
    second_half = vectors[..., half_dim:]
    return jnp.concatenate(
        [
            first_half * cosine - second_half * sine_part,
            second_half * cosine + first_half * sine_part,
        ],
        -1,
    )


def attend(turned, cache_keys, cache_values, fresh_keys, fresh_values, lengths):
    score_scale = 1.0 / math.sqrt(turned.shape[-1])
    slot_count = cache_keys.shape[1]
    cached = (
        jnp.einsum("rhd,rld->rhl", turned, cache_keys, preferred_element_type=jnp.float32)
        * score_scale
    )
    usable = lax.broadcasted_iota(jnp.int32, (turned.shape[0], slot_count), 1) < lengths[:, None]
    cached = jnp.where(usable[:, None, :], cached, -1e30)
    recent = (
        jnp.einsum("rhd,rnd->rhn", turned, fresh_keys, preferred_element_type=jnp.float32)
        * score_scale
    )
    scores = jnp.concatenate([cached, recent], -1)
    row_max = jnp.max(scores, -1, keepdims=True)
    shifted = jnp.exp(scores - row_max)
    weights = (shifted / jnp.sum(shifted, -1, keepdims=True)).astype(jnp.bfloat16)
    mixture = jnp.einsum(
        "rhl,rld->rhd", weights[..., :slot_count], cache_values, preferred_element_type=jnp.float32
    )
    mixture = mixture + jnp.einsum(
        "rhn,rnd->rhd", weights[..., slot_count:], fresh_values, preferred_element_type=jnp.float32
    )
    return mixture.astype(jnp.bfloat16)


def per_device(
    queries,
    new_kv,
    cache,
    lengths,
    positions,
    hidden,
    norm_gain,
    route_ids,
    route_weight,
    w_gate_up,
    w_down,
):
    step_count = queries.shape[0]
    requests = queries.shape[1]
    head_dim = cache.shape[-1]
    head_count = queries.shape[2] // head_dim
    turned_keys = [
        rotate(new_kv[step_at, 0][:, None, :].astype(jnp.float32), positions[step_at])[:, 0, :]
        for step_at in range(step_count)
    ]
    fresh_keys = jnp.stack(turned_keys, 1).astype(jnp.bfloat16)
    fresh_values = jnp.transpose(new_kv[:, 1], (1, 0, 2))
    attention = []
    for step_at in range(step_count):
        turned = rotate(
            queries[step_at].reshape(requests, head_count, head_dim).astype(jnp.float32),
            positions[step_at],
        )
        turned = turned.astype(jnp.bfloat16)
        mixture = attend(
            turned,
            cache[0],
            cache[1],
            fresh_keys[:, : step_at + 1],
            fresh_values[:, : step_at + 1],
            lengths,
        )
        attention.append(mixture.reshape(requests, head_count * head_dim))
    attention = jnp.stack(attention)
    owners = lax.axis_size("dp")
    groups = lax.axis_size("head")
    local_experts = w_down.shape[0]
    experts = owners * local_experts
    top_count = route_ids.shape[-1]
    slot_count = max(2, requests * top_count // experts)
    model_width = norm_gain.shape[0]
    hidden_part = w_down.shape[1]
    chunk = hidden.shape[-1]
    tokens = step_count * requests
    slots = step_count * slot_count

    slot_of = []
    for step_at in range(step_count):
        flat_ids = route_ids[step_at].reshape(-1)
        onehot = (
            flat_ids[:, None] == lax.broadcasted_iota(jnp.int32, (flat_ids.shape[0], experts), 1)
        ).astype(jnp.int32)
        rank_in = jnp.sum((jnp.cumsum(onehot, 0) - onehot) * onehot, 1)
        slot_of.append((flat_ids * slots + step_at * slot_count + rank_in).reshape(requests, top_count))
    slot_of = jnp.concatenate(slot_of, 0)
    slot_grid = lax.broadcasted_iota(jnp.int32, (experts, slots, tokens, top_count), 0) * slots + (
        lax.broadcasted_iota(jnp.int32, (experts, slots, tokens, top_count), 1)
    )
    hit = slot_grid == slot_of[None, None]
    placement = jnp.any(hit, 3).astype(jnp.bfloat16)
    own_rows = hidden.reshape(tokens, chunk)
    outgoing = jnp.einsum(
        "ejt,tf->ejf", placement, own_rows, preferred_element_type=jnp.float32
    ).astype(jnp.bfloat16)
    received = lax.all_to_all(outgoing, "dp", split_axis=0, concat_axis=0, tiled=True)
    received = received.reshape(experts * slots, chunk)
    assert groups == 4
    me = lax.axis_index("head")
    to_right = [(j, (j + 1) % groups) for j in range(groups)]
    to_left = [(j, (j - 1) % groups) for j in range(groups)]
    half = received.shape[0] // 2

    def ring_sum(terms, plus):
        half = terms[0].shape[0] // 2
        far_a = lax.ppermute(terms[2][:half], "head", to_right)
        far_b = lax.ppermute(terms[2][half:], "head", to_left)
        near_r = lax.ppermute(
            jnp.concatenate([plus(terms[1][:half], far_a), terms[1][half:]], 0), "head", to_right
        )
        near_l = lax.ppermute(
            jnp.concatenate([terms[3][:half], plus(terms[3][half:], far_b)], 0), "head", to_left
        )
        return plus(plus(terms[0], near_r), near_l)

    up_cols = w_gate_up[0]
    up_blocks = [lax.dynamic_slice_in_dim(up_cols, me * chunk, chunk, 0)]
    for k in range(1, groups):
        piece = lax.dynamic_slice_in_dim(up_cols, ((me - k) % groups) * chunk, chunk, 0)
        up_blocks.append(lax.ppermute(piece, "head", [(j, (j - k) % groups) for j in range(groups)]))
    own_gain = lax.dynamic_slice_in_dim(norm_gain, me * chunk, chunk).astype(jnp.float32)
    wide = received.astype(jnp.float32)
    row_count = received.shape[0]
    up_width = 2 * hidden_part
    extra_rows = 16
    square_sums = jnp.pad(
        jnp.sum(wide * wide, 1), (0, extra_rows * up_width - row_count)
    ).reshape(extra_rows, up_width)
    scaled = (wide * own_gain[None, :]).astype(jnp.bfloat16)
    shares_of_up = jnp.einsum(
        "rf,kfc->krc", scaled, jnp.stack(up_blocks), preferred_element_type=jnp.float32
    )
    reduced = ring_sum(
        [jnp.concatenate([shares_of_up[k], square_sums], 0) for k in range(groups)],
        lambda a, b: a + b,
    )
    mean_sq = reduced[row_count:].reshape(-1)[:row_count] / model_width
    gate_up = reduced[:row_count] * lax.rsqrt(mean_sq + EPS)[:, None]
    activated = (jax.nn.silu(gate_up[:, :hidden_part]) * gate_up[:, hidden_part:]).astype(
        jnp.bfloat16
    )
    quarter_at = [(me + k) % groups for k in range(groups)]
    partial_out = [
        jnp.dot(
            activated,
            lax.dynamic_slice_in_dim(w_down[0], q * chunk, chunk, 1),
            preferred_element_type=jnp.float32,
        ).astype(jnp.bfloat16)
        for q in quarter_at
    ]

    def plus(a, b):
        return (a.astype(jnp.float32) + b.astype(jnp.float32)).astype(jnp.bfloat16)

    summed = ring_sum(partial_out, plus)
    returned = lax.all_to_all(
        summed.reshape(experts, slots, chunk), "dp", split_axis=0, concat_axis=0, tiled=True
    )

    shares = route_weight / jnp.sum(route_weight, -1, keepdims=True)
    combine = jnp.sum(
        jnp.where(hit, shares.reshape(1, 1, tokens, top_count), 0.0), 3
    )
    contrib = jnp.einsum(
        "ejt,ejf->tf",
        combine,
        returned.astype(jnp.float32),
        precision=lax.Precision.HIGHEST,
        preferred_element_type=jnp.float32,
    )
    layer_out = (own_rows.astype(jnp.float32) + contrib).astype(jnp.bfloat16)
    layer_out = layer_out.reshape(step_count, requests, chunk)
    return (attention, layer_out)


def solution(mesh):
    return jax.shard_map(
        per_device,
        mesh=mesh,
        in_specs=(
            P(None, "dp", "head"),
            P(None, None, "dp", "head"),
            P(None, "dp", None, "head"),
            P("dp"),
            P(None, None, "dp"),
            P(None, "dp", "head"),
            P(),
            P(None, "dp", None),
            P(None, "dp", None),
            P("dp", None, "head"),
            P("dp", "head", None),
        ),
        out_specs=(P(None, "dp", "head"), P(None, "dp", "head")),
        check_vma=False,
    )
```

```python
import math

import jax
import jax.numpy as jnp
from jax import lax
from jax.sharding import PartitionSpec as P

EPS = 1e-06
ROPE_BASE = 5000000.0


def rotate(vectors, pos_ids):
    head_size = vectors.shape[-1]
    half_dim = head_size // 2
    freq_index = jnp.arange(half_dim, dtype=jnp.int32)
    inverse_freq = jnp.exp(
        freq_index.astype(jnp.float32) * (-2.0 * math.log(ROPE_BASE) / head_size)
    )
    alternated = 60 * half_dim // 64
    axis_pick = jnp.where(freq_index < alternated, freq_index % 3, 0)
    pos_float = pos_ids.astype(jnp.float32)
    chosen = jnp.where(
        axis_pick[None, :] == 0,
        pos_float[0][:, None],
        jnp.where(axis_pick[None, :] == 1, pos_float[1][:, None], pos_float[2][:, None]),
    )
    angles = chosen * inverse_freq[None, :]
    cosine = jnp.cos(angles)[:, None, :]
    sine_part = jnp.sin(angles)[:, None, :]
    first_half = vectors[..., :half_dim]
    second_half = vectors[..., half_dim:]
    return jnp.concatenate(
        [
            first_half * cosine - second_half * sine_part,
            second_half * cosine + first_half * sine_part,
        ],
        -1,
    )


def attend(turned, cache_keys, cache_values, fresh_keys, fresh_values, lengths):
    score_scale = 1.0 / math.sqrt(turned.shape[-1])
    slot_count = cache_keys.shape[1]
    cached = (
        jnp.einsum("rhd,rld->rhl", turned, cache_keys, preferred_element_type=jnp.float32)
        * score_scale
    )
    usable = lax.broadcasted_iota(jnp.int32, (turned.shape[0], slot_count), 1) < lengths[:, None]
    cached = jnp.where(usable[:, None, :], cached, -1e30)
    recent = (
        jnp.einsum("rhd,rnd->rhn", turned, fresh_keys, preferred_element_type=jnp.float32)
        * score_scale
    )
    scores = jnp.concatenate([cached, recent], -1)
    row_max = jnp.max(scores, -1, keepdims=True)
    shifted = jnp.exp(scores - row_max)
    weights = (shifted / jnp.sum(shifted, -1, keepdims=True)).astype(jnp.bfloat16)
    mixture = jnp.einsum(
        "rhl,rld->rhd", weights[..., :slot_count], cache_values, preferred_element_type=jnp.float32
    )
    mixture = mixture + jnp.einsum(
        "rhn,rnd->rhd", weights[..., slot_count:], fresh_values, preferred_element_type=jnp.float32
    )
    return mixture.astype(jnp.bfloat16)


def per_device(
    queries,
    new_kv,
    cache,
    lengths,
    positions,
    hidden,
    norm_gain,
    route_ids,
    route_weight,
    w_gate_up,
    w_down,
):
    step_count = queries.shape[0]
    requests = queries.shape[1]
    head_dim = cache.shape[-1]
    head_count = queries.shape[2] // head_dim
    turned_keys = [
        rotate(new_kv[step_at, 0][:, None, :].astype(jnp.float32), positions[step_at])[:, 0, :]
        for step_at in range(step_count)
    ]
    fresh_keys = jnp.stack(turned_keys, 1).astype(jnp.bfloat16)
    fresh_values = jnp.transpose(new_kv[:, 1], (1, 0, 2))
    attention = []
    for step_at in range(step_count):
        turned = rotate(
            queries[step_at].reshape(requests, head_count, head_dim).astype(jnp.float32),
            positions[step_at],
        )
        turned = turned.astype(jnp.bfloat16)
        mixture = attend(
            turned,
            cache[0],
            cache[1],
            fresh_keys[:, : step_at + 1],
            fresh_values[:, : step_at + 1],
            lengths,
        )
        attention.append(mixture.reshape(requests, head_count * head_dim))
    attention = jnp.stack(attention)
    owners = lax.axis_size("dp")
    groups = lax.axis_size("head")
    local_experts = w_down.shape[0]
    experts = owners * local_experts
    top_count = route_ids.shape[-1]
    slot_count = max(2, requests * top_count // experts)
    model_width = norm_gain.shape[0]
    hidden_part = w_down.shape[1]
    chunk = hidden.shape[-1]
    tokens = step_count * requests
    slots = step_count * slot_count

    slot_of = []
    for step_at in range(step_count):
        flat_ids = route_ids[step_at].reshape(-1)
        onehot = (
            flat_ids[:, None] == lax.broadcasted_iota(jnp.int32, (flat_ids.shape[0], experts), 1)
        ).astype(jnp.int32)
        rank_in = jnp.sum((jnp.cumsum(onehot, 0) - onehot) * onehot, 1)
        slot_of.append((flat_ids * slots + step_at * slot_count + rank_in).reshape(requests, top_count))
    slot_of = jnp.concatenate(slot_of, 0)
    slot_grid = lax.broadcasted_iota(jnp.int32, (experts, slots, tokens, top_count), 0) * slots + (
        lax.broadcasted_iota(jnp.int32, (experts, slots, tokens, top_count), 1)
    )
    hit = slot_grid == slot_of[None, None]
    placement = jnp.any(hit, 3).astype(jnp.bfloat16)
    own_rows = hidden.reshape(tokens, chunk)
    outgoing = jnp.einsum(
        "ejt,tf->ejf", placement, own_rows, preferred_element_type=jnp.float32
    ).astype(jnp.bfloat16)
    received = lax.all_to_all(outgoing, "dp", split_axis=0, concat_axis=0, tiled=True)
    received = received.reshape(experts * slots, chunk)
    assert groups == 4
    me = lax.axis_index("head")
    to_right = [(j, (j + 1) % groups) for j in range(groups)]
    to_left = [(j, (j - 1) % groups) for j in range(groups)]
    half = received.shape[0] // 2

    def ring_sum(terms, plus):
        far_a = lax.ppermute(terms[2][:half], "head", to_right)
        far_b = lax.ppermute(terms[2][half:], "head", to_left)
        near_r = lax.ppermute(
            jnp.concatenate([plus(terms[1][:half], far_a), terms[1][half:]], 0), "head", to_right
        )
        near_l = lax.ppermute(
            jnp.concatenate([terms[3][:half], plus(terms[3][half:], far_b)], 0), "head", to_left
        )
        return plus(plus(terms[0], near_r), near_l)

    up_cols = w_gate_up[0]
    up_blocks = [lax.dynamic_slice_in_dim(up_cols, me * chunk, chunk, 0)]
    for k in range(1, groups):
        piece = lax.dynamic_slice_in_dim(up_cols, ((me - k) % groups) * chunk, chunk, 0)
        up_blocks.append(lax.ppermute(piece, "head", [(j, (j - k) % groups) for j in range(groups)]))
    down_rows = w_down[0]
    down_blocks = [lax.dynamic_slice_in_dim(down_rows, me * chunk, chunk, 1)]
    for k in range(1, groups):
        piece = lax.dynamic_slice_in_dim(down_rows, ((me - k) % groups) * chunk, chunk, 1)
        down_blocks.append(
            lax.ppermute(piece, "head", [(j, (j - k) % groups) for j in range(groups)])
        )
    own_gain = lax.dynamic_slice_in_dim(norm_gain, me * chunk, chunk).astype(jnp.float32)
    wide = received.astype(jnp.float32)
    mean_sq = lax.psum(jnp.sum(wide * wide, 1), "head") / model_width
    scaled = (wide * own_gain[None, :]).astype(jnp.bfloat16)
    shares_of_up = jnp.einsum(
        "rf,kfc->krc", scaled, jnp.stack(up_blocks), preferred_element_type=jnp.float32
    )
    gate_up = ring_sum([shares_of_up[k] for k in range(groups)], lambda a, b: a + b)
    gate_up = gate_up * lax.rsqrt(mean_sq + EPS)[:, None]
    activated = (jax.nn.silu(gate_up[:, :hidden_part]) * gate_up[:, hidden_part:]).astype(
        jnp.bfloat16
    )
    act_half = activated.shape[0] // 2
    act_left = lax.ppermute(activated, "head", to_right)
    act_right = lax.ppermute(activated, "head", to_left)
    act_far = jnp.concatenate(
        [
            lax.ppermute(act_left[:act_half], "head", to_right),
            lax.ppermute(act_right[act_half:], "head", to_left),
        ],
        0,
    )
    act_blocks = [activated, act_right, act_far, act_left]
    summed = None
    for act_block, down_block in zip(act_blocks, down_blocks):
        part = (
            jnp.dot(act_block, down_block, preferred_element_type=jnp.float32)
            .astype(jnp.bfloat16)
            .astype(jnp.float32)
        )
        summed = part if summed is None else summed + part
    summed = summed.astype(jnp.bfloat16)
    returned = lax.all_to_all(
        summed.reshape(experts, slots, chunk), "dp", split_axis=0, concat_axis=0, tiled=True
    )

    shares = route_weight / jnp.sum(route_weight, -1, keepdims=True)
    combine = jnp.sum(
        jnp.where(hit, shares.reshape(1, 1, tokens, top_count), 0.0), 3
    )
    contrib = jnp.einsum(
        "ejt,ejf->tf",
        combine,
        returned.astype(jnp.float32),
        precision=lax.Precision.HIGHEST,
        preferred_element_type=jnp.float32,
    )
    layer_out = (own_rows.astype(jnp.float32) + contrib).astype(jnp.bfloat16)
    layer_out = layer_out.reshape(step_count, requests, chunk)
    return (attention, layer_out)


def solution(mesh):
    return jax.shard_map(
        per_device,
        mesh=mesh,
        in_specs=(
            P(None, "dp", "head"),
            P(None, None, "dp", "head"),
            P(None, "dp", None, "head"),
            P("dp"),
            P(None, None, "dp"),
            P(None, "dp", "head"),
            P(),
            P(None, "dp", None),
            P(None, "dp", None),
            P("dp", None, "head"),
            P("dp", "head", None),
        ),
        out_specs=(P(None, "dp", "head"), P(None, "dp", "head")),
        check_vma=False,
    )
```

```python
import math

import jax
import jax.numpy as jnp
from jax import lax
from jax.sharding import PartitionSpec as P

EPS = 1e-06
ROPE_BASE = 5000000.0


def rotate(vectors, pos_ids):
    head_size = vectors.shape[-1]
    half_dim = head_size // 2
    freq_index = jnp.arange(half_dim, dtype=jnp.int32)
    inverse_freq = jnp.exp(
        freq_index.astype(jnp.float32) * (-2.0 * math.log(ROPE_BASE) / head_size)
    )
    alternated = 60 * half_dim // 64
    axis_pick = jnp.where(freq_index < alternated, freq_index % 3, 0)
    pos_float = pos_ids.astype(jnp.float32)
    chosen = jnp.where(
        axis_pick[None, :] == 0,
        pos_float[0][:, None],
        jnp.where(axis_pick[None, :] == 1, pos_float[1][:, None], pos_float[2][:, None]),
    )
    angles = chosen * inverse_freq[None, :]
    cosine = jnp.cos(angles)[:, None, :]
    sine_part = jnp.sin(angles)[:, None, :]
    first_half = vectors[..., :half_dim]
    second_half = vectors[..., half_dim:]
    return jnp.concatenate(
        [
            first_half * cosine - second_half * sine_part,
            second_half * cosine + first_half * sine_part,
        ],
        -1,
    )


def attend(turned, cache_keys, cache_values, fresh_keys, fresh_values, lengths):
    score_scale = 1.0 / math.sqrt(turned.shape[-1])
    slot_count = cache_keys.shape[1]
    cached = (
        jnp.einsum("rhd,rld->rhl", turned, cache_keys, preferred_element_type=jnp.float32)
        * score_scale
    )
    usable = lax.broadcasted_iota(jnp.int32, (turned.shape[0], slot_count), 1) < lengths[:, None]
    cached = jnp.where(usable[:, None, :], cached, -1e30)
    recent = (
        jnp.einsum("rhd,rnd->rhn", turned, fresh_keys, preferred_element_type=jnp.float32)
        * score_scale
    )
    scores = jnp.concatenate([cached, recent], -1)
    row_max = jnp.max(scores, -1, keepdims=True)
    shifted = jnp.exp(scores - row_max)
    weights = (shifted / jnp.sum(shifted, -1, keepdims=True)).astype(jnp.bfloat16)
    mixture = jnp.einsum(
        "rhl,rld->rhd", weights[..., :slot_count], cache_values, preferred_element_type=jnp.float32
    )
    mixture = mixture + jnp.einsum(
        "rhn,rnd->rhd", weights[..., slot_count:], fresh_values, preferred_element_type=jnp.float32
    )
    return mixture.astype(jnp.bfloat16)


def per_device(
    queries,
    new_kv,
    cache,
    lengths,
    positions,
    hidden,
    norm_gain,
    route_ids,
    route_weight,
    w_gate_up,
    w_down,
):
    step_count = queries.shape[0]
    requests = queries.shape[1]
    head_dim = cache.shape[-1]
    head_count = queries.shape[2] // head_dim
    turned_keys = [
        rotate(new_kv[step_at, 0][:, None, :].astype(jnp.float32), positions[step_at])[:, 0, :]
        for step_at in range(step_count)
    ]
    fresh_keys = jnp.stack(turned_keys, 1).astype(jnp.bfloat16)
    fresh_values = jnp.transpose(new_kv[:, 1], (1, 0, 2))
    attention = []
    for step_at in range(step_count):
        turned = rotate(
            queries[step_at].reshape(requests, head_count, head_dim).astype(jnp.float32),
            positions[step_at],
        )
        turned = turned.astype(jnp.bfloat16)
        mixture = attend(
            turned,
            cache[0],
            cache[1],
            fresh_keys[:, : step_at + 1],
            fresh_values[:, : step_at + 1],
            lengths,
        )
        attention.append(mixture.reshape(requests, head_count * head_dim))
    attention = jnp.stack(attention)
    owners = lax.axis_size("dp")
    groups = lax.axis_size("head")
    local_experts = w_down.shape[0]
    experts = owners * local_experts
    top_count = route_ids.shape[-1]
    slot_count = max(2, requests * top_count // experts)
    model_width = norm_gain.shape[0]
    hidden_part = w_down.shape[1]
    chunk = hidden.shape[-1]
    tokens = step_count * requests
    slots = step_count * slot_count

    slot_of = []
    for step_at in range(step_count):
        flat_ids = route_ids[step_at].reshape(-1)
        onehot = (
            flat_ids[:, None] == lax.broadcasted_iota(jnp.int32, (flat_ids.shape[0], experts), 1)
        ).astype(jnp.int32)
        rank_in = jnp.sum((jnp.cumsum(onehot, 0) - onehot) * onehot, 1)
        slot_of.append((flat_ids * slots + step_at * slot_count + rank_in).reshape(requests, top_count))
    slot_of = jnp.concatenate(slot_of, 0)
    slot_grid = lax.broadcasted_iota(jnp.int32, (experts, slots, tokens, top_count), 0) * slots + (
        lax.broadcasted_iota(jnp.int32, (experts, slots, tokens, top_count), 1)
    )
    hit = slot_grid == slot_of[None, None]
    placement = jnp.any(hit, 3).astype(jnp.bfloat16)
    own_rows = hidden.reshape(tokens, chunk)
    outgoing = jnp.einsum(
        "ejt,tf->ejf", placement, own_rows, preferred_element_type=jnp.float32
    ).astype(jnp.bfloat16)
    received = lax.all_to_all(outgoing, "dp", split_axis=0, concat_axis=0, tiled=True)
    received = received.reshape(experts * slots, chunk)
    assert groups == 4
    me = lax.axis_index("head")
    to_right = [(j, (j + 1) % groups) for j in range(groups)]
    to_left = [(j, (j - 1) % groups) for j in range(groups)]
    half = received.shape[0] // 2

    def ring_sum(terms, plus, side):
        far_a = lax.ppermute(terms[2][:half], "head", to_right)
        far_b = lax.ppermute(terms[2][half:], "head", to_left)
        side_left = lax.ppermute(side, "head", to_right)
        side_right = lax.ppermute(side, "head", to_left)
        near_r = lax.ppermute(
            jnp.concatenate([plus(terms[1][:half], far_a), terms[1][half:]], 0), "head", to_right
        )
        near_l = lax.ppermute(
            jnp.concatenate([terms[3][:half], plus(terms[3][half:], far_b)], 0), "head", to_left
        )
        side_far = lax.ppermute(side + side_left, "head", to_right)
        return plus(plus(terms[0], near_r), near_l), side + side_right + side_far

    up_cols = w_gate_up[0]
    up_blocks = [lax.dynamic_slice_in_dim(up_cols, me * chunk, chunk, 0)]
    for k in range(1, groups):
        piece = lax.dynamic_slice_in_dim(up_cols, ((me - k) % groups) * chunk, chunk, 0)
        up_blocks.append(lax.ppermute(piece, "head", [(j, (j - k) % groups) for j in range(groups)]))
    down_rows = w_down[0]
    down_blocks = [lax.dynamic_slice_in_dim(down_rows, me * chunk, chunk, 1)]
    for k in range(1, groups):
        piece = lax.dynamic_slice_in_dim(down_rows, ((me - k) % groups) * chunk, chunk, 1)
        down_blocks.append(
            lax.ppermute(piece, "head", [(j, (j - k) % groups) for j in range(groups)])
        )
    own_gain = lax.dynamic_slice_in_dim(norm_gain, me * chunk, chunk).astype(jnp.float32)
    wide = received.astype(jnp.float32)
    square_sums = jnp.sum(wide * wide, 1)
    scaled = (wide * own_gain[None, :]).astype(jnp.bfloat16)
    shares_of_up = jnp.einsum(
        "rf,kfc->krc", scaled, jnp.stack(up_blocks), preferred_element_type=jnp.float32
    )
    gate_up, square_sums = ring_sum(
        [shares_of_up[k] for k in range(groups)], lambda a, b: a + b, square_sums
    )
    mean_sq = square_sums / model_width
    gate_up = gate_up * lax.rsqrt(mean_sq + EPS)[:, None]
    activated = (jax.nn.silu(gate_up[:, :hidden_part]) * gate_up[:, hidden_part:]).astype(
        jnp.bfloat16
    )
    act_half = activated.shape[0] // 2
    act_left = lax.ppermute(activated, "head", to_right)
    act_right = lax.ppermute(activated, "head", to_left)
    act_far = jnp.concatenate(
        [
            lax.ppermute(act_left[:act_half], "head", to_right),
            lax.ppermute(act_right[act_half:], "head", to_left),
        ],
        0,
    )
    act_blocks = [activated, act_right, act_far, act_left]
    summed = None
    for act_block, down_block in zip(act_blocks, down_blocks):
        part = (
            jnp.dot(act_block, down_block, preferred_element_type=jnp.float32)
            .astype(jnp.bfloat16)
            .astype(jnp.float32)
        )
        summed = part if summed is None else summed + part
    summed = summed.astype(jnp.bfloat16)
    returned = lax.all_to_all(
        summed.reshape(experts, slots, chunk), "dp", split_axis=0, concat_axis=0, tiled=True
    )

    shares = route_weight / jnp.sum(route_weight, -1, keepdims=True)
    combine = jnp.sum(
        jnp.where(hit, shares.reshape(1, 1, tokens, top_count), 0.0), 3
    )
    contrib = jnp.einsum(
        "ejt,ejf->tf",
        combine,
        returned.astype(jnp.float32),
        precision=lax.Precision.HIGHEST,
        preferred_element_type=jnp.float32,
    )
    layer_out = (own_rows.astype(jnp.float32) + contrib).astype(jnp.bfloat16)
    layer_out = layer_out.reshape(step_count, requests, chunk)
    return (attention, layer_out)


def solution(mesh):
    return jax.shard_map(
        per_device,
        mesh=mesh,
        in_specs=(
            P(None, "dp", "head"),
            P(None, None, "dp", "head"),
            P(None, "dp", None, "head"),
            P("dp"),
            P(None, None, "dp"),
            P(None, "dp", "head"),
            P(),
            P(None, "dp", None),
            P(None, "dp", None),
            P("dp", None, "head"),
            P("dp", "head", None),
        ),
        out_specs=(P(None, "dp", "head"), P(None, "dp", "head")),
        check_vma=False,
    )
```

```python
import math

import jax
import jax.numpy as jnp
from jax import lax
from jax.sharding import PartitionSpec as P

EPS = 1e-06
ROPE_BASE = 5000000.0


def rotate(vectors, pos_ids):
    head_size = vectors.shape[-1]
    half_dim = head_size // 2
    freq_index = jnp.arange(half_dim, dtype=jnp.int32)
    inverse_freq = jnp.exp(
        freq_index.astype(jnp.float32) * (-2.0 * math.log(ROPE_BASE) / head_size)
    )
    alternated = 60 * half_dim // 64
    axis_pick = jnp.where(freq_index < alternated, freq_index % 3, 0)
    pos_float = pos_ids.astype(jnp.float32)
    chosen = jnp.where(
        axis_pick[None, :] == 0,
        pos_float[0][:, None],
        jnp.where(axis_pick[None, :] == 1, pos_float[1][:, None], pos_float[2][:, None]),
    )
    angles = chosen * inverse_freq[None, :]
    cosine = jnp.cos(angles)[:, None, :]
    sine_part = jnp.sin(angles)[:, None, :]
    first_half = vectors[..., :half_dim]
    second_half = vectors[..., half_dim:]
    return jnp.concatenate(
        [
            first_half * cosine - second_half * sine_part,
            second_half * cosine + first_half * sine_part,
        ],
        -1,
    )


def attend(turned, cache_keys, cache_values, fresh_keys, fresh_values, lengths):
    score_scale = 1.0 / math.sqrt(turned.shape[-1])
    slot_count = cache_keys.shape[1]
    cached = (
        jnp.einsum("rhd,rld->rhl", turned, cache_keys, preferred_element_type=jnp.float32)
        * score_scale
    )
    usable = lax.broadcasted_iota(jnp.int32, (turned.shape[0], slot_count), 1) < lengths[:, None]
    cached = jnp.where(usable[:, None, :], cached, -1e30)
    recent = (
        jnp.einsum("rhd,rnd->rhn", turned, fresh_keys, preferred_element_type=jnp.float32)
        * score_scale
    )
    scores = jnp.concatenate([cached, recent], -1)
    row_max = jnp.max(scores, -1, keepdims=True)
    shifted = jnp.exp(scores - row_max)
    weights = (shifted / jnp.sum(shifted, -1, keepdims=True)).astype(jnp.bfloat16)
    mixture = jnp.einsum(
        "rhl,rld->rhd", weights[..., :slot_count], cache_values, preferred_element_type=jnp.float32
    )
    mixture = mixture + jnp.einsum(
        "rhn,rnd->rhd", weights[..., slot_count:], fresh_values, preferred_element_type=jnp.float32
    )
    return mixture.astype(jnp.bfloat16)


def per_device(
    queries,
    new_kv,
    cache,
    lengths,
    positions,
    hidden,
    norm_gain,
    route_ids,
    route_weight,
    w_gate_up,
    w_down,
):
    step_count = queries.shape[0]
    requests = queries.shape[1]
    head_dim = cache.shape[-1]
    head_count = queries.shape[2] // head_dim
    turned_keys = [
        rotate(new_kv[step_at, 0][:, None, :].astype(jnp.float32), positions[step_at])[:, 0, :]
        for step_at in range(step_count)
    ]
    fresh_keys = jnp.stack(turned_keys, 1).astype(jnp.bfloat16)
    fresh_values = jnp.transpose(new_kv[:, 1], (1, 0, 2))
    attention = []
    for step_at in range(step_count):
        turned = rotate(
            queries[step_at].reshape(requests, head_count, head_dim).astype(jnp.float32),
            positions[step_at],
        )
        turned = turned.astype(jnp.bfloat16)
        mixture = attend(
            turned,
            cache[0],
            cache[1],
            fresh_keys[:, : step_at + 1],
            fresh_values[:, : step_at + 1],
            lengths,
        )
        attention.append(mixture.reshape(requests, head_count * head_dim))
    attention = jnp.stack(attention)
    owners = lax.axis_size("dp")
    groups = lax.axis_size("head")
    local_experts = w_down.shape[0]
    experts = owners * local_experts
    top_count = route_ids.shape[-1]
    slot_count = max(2, requests * top_count // experts)
    model_width = norm_gain.shape[0]
    hidden_part = w_down.shape[1]
    chunk = hidden.shape[-1]
    tokens = step_count * requests
    slots = step_count * slot_count

    slot_of = []
    for step_at in range(step_count):
        flat_ids = route_ids[step_at].reshape(-1)
        onehot = (
            flat_ids[:, None] == lax.broadcasted_iota(jnp.int32, (flat_ids.shape[0], experts), 1)
        ).astype(jnp.int32)
        rank_in = jnp.sum((jnp.cumsum(onehot, 0) - onehot) * onehot, 1)
        slot_of.append((flat_ids * slots + step_at * slot_count + rank_in).reshape(requests, top_count))
    slot_of = jnp.concatenate(slot_of, 0)
    slot_grid = lax.broadcasted_iota(jnp.int32, (experts, slots, tokens, top_count), 0) * slots + (
        lax.broadcasted_iota(jnp.int32, (experts, slots, tokens, top_count), 1)
    )
    hit = slot_grid == slot_of[None, None]
    placement = jnp.any(hit, 3).astype(jnp.bfloat16)
    own_rows = hidden.reshape(tokens, chunk)
    outgoing = jnp.einsum(
        "ejt,tf->ejf", placement, own_rows, preferred_element_type=jnp.float32
    ).astype(jnp.bfloat16)
    received = lax.all_to_all(outgoing, "dp", split_axis=0, concat_axis=0, tiled=True)
    received = received.reshape(experts * slots, chunk)
    assert groups == 4
    me = lax.axis_index("head")
    to_right = [(j, (j + 1) % groups) for j in range(groups)]
    to_left = [(j, (j - 1) % groups) for j in range(groups)]
    half = received.shape[0] // 2

    def ring_sum(terms, plus, side):
        far_a = lax.ppermute(terms[2][:half], "head", to_right)
        far_b = lax.ppermute(terms[2][half:], "head", to_left)
        side_left = lax.ppermute(side, "head", to_right)
        side_right = lax.ppermute(side, "head", to_left)
        near_r = lax.ppermute(
            jnp.concatenate([plus(terms[1][:half], far_a), terms[1][half:]], 0), "head", to_right
        )
        near_l = lax.ppermute(
            jnp.concatenate([terms[3][:half], plus(terms[3][half:], far_b)], 0), "head", to_left
        )
        side_far = lax.ppermute(side + side_left, "head", to_right)
        return plus(plus(terms[0], near_r), near_l), side + side_right + side_far

    up_cols = w_gate_up[0]
    up_blocks = [lax.dynamic_slice_in_dim(up_cols, me * chunk, chunk, 0)]
    for k in range(1, groups):
        piece = lax.dynamic_slice_in_dim(up_cols, ((me - k) % groups) * chunk, chunk, 0)
        up_blocks.append(lax.ppermute(piece, "head", [(j, (j - k) % groups) for j in range(groups)]))
    down_rows = w_down[0]
    down_blocks = [lax.dynamic_slice_in_dim(down_rows, me * chunk, chunk, 1)]
    for k in range(1, groups):
        piece = lax.dynamic_slice_in_dim(down_rows, ((me - k) % groups) * chunk, chunk, 1)
        down_blocks.append(
            lax.ppermute(piece, "head", [(j, (j - k) % groups) for j in range(groups)])
        )
    own_gain = lax.dynamic_slice_in_dim(norm_gain, me * chunk, chunk).astype(jnp.float32)
    wide = received.astype(jnp.float32)
    square_sums = jnp.sum(wide * wide, 1)
    scaled = (wide * own_gain[None, :]).astype(jnp.bfloat16)
    shares_of_up = jnp.einsum(
        "rf,kfc->krc", scaled, jnp.stack(up_blocks), preferred_element_type=jnp.float32
    )
    gate_up, square_sums = ring_sum(
        [shares_of_up[k] for k in range(groups)], lambda a, b: a + b, square_sums
    )
    mean_sq = square_sums / model_width
    gate_up = gate_up * lax.rsqrt(mean_sq + EPS)[:, None]
    activated = (jax.nn.silu(gate_up[:, :hidden_part]) * gate_up[:, hidden_part:]).astype(
        jnp.bfloat16
    )
    act_left = lax.ppermute(activated, "head", to_right)
    act_right = lax.ppermute(activated, "head", to_left)
    act_far = lax.ppermute(act_left, "head", to_right)
    act_blocks = [activated, act_right, act_far, act_left]
    summed = None
    for act_block, down_block in zip(act_blocks, down_blocks):
        part = (
            jnp.dot(act_block, down_block, preferred_element_type=jnp.float32)
            .astype(jnp.bfloat16)
            .astype(jnp.float32)
        )
        summed = part if summed is None else summed + part
    summed = summed.astype(jnp.bfloat16)
    returned = lax.all_to_all(
        summed.reshape(experts, slots, chunk), "dp", split_axis=0, concat_axis=0, tiled=True
    )

    shares = route_weight / jnp.sum(route_weight, -1, keepdims=True)
    combine = jnp.sum(
        jnp.where(hit, shares.reshape(1, 1, tokens, top_count), 0.0), 3
    )
    contrib = jnp.einsum(
        "ejt,ejf->tf",
        combine,
        returned.astype(jnp.float32),
        precision=lax.Precision.HIGHEST,
        preferred_element_type=jnp.float32,
    )
    layer_out = (own_rows.astype(jnp.float32) + contrib).astype(jnp.bfloat16)
    layer_out = layer_out.reshape(step_count, requests, chunk)
    return (attention, layer_out)


def solution(mesh):
    return jax.shard_map(
        per_device,
        mesh=mesh,
        in_specs=(
            P(None, "dp", "head"),
            P(None, None, "dp", "head"),
            P(None, "dp", None, "head"),
            P("dp"),
            P(None, None, "dp"),
            P(None, "dp", "head"),
            P(),
            P(None, "dp", None),
            P(None, "dp", None),
            P("dp", None, "head"),
            P("dp", "head", None),
        ),
        out_specs=(P(None, "dp", "head"), P(None, "dp", "head")),
        check_vma=False,
    )
```

```python
import math

import jax
import jax.numpy as jnp
from jax import lax
from jax.sharding import PartitionSpec as P

EPS = 1e-06
ROPE_BASE = 5000000.0


def rotate(vectors, pos_ids):
    head_size = vectors.shape[-1]
    half_dim = head_size // 2
    freq_index = jnp.arange(half_dim, dtype=jnp.int32)
    inverse_freq = jnp.exp(
        freq_index.astype(jnp.float32) * (-2.0 * math.log(ROPE_BASE) / head_size)
    )
    alternated = 60 * half_dim // 64
    axis_pick = jnp.where(freq_index < alternated, freq_index % 3, 0)
    pos_float = pos_ids.astype(jnp.float32)
    chosen = jnp.where(
        axis_pick[None, :] == 0,
        pos_float[0][:, None],
        jnp.where(axis_pick[None, :] == 1, pos_float[1][:, None], pos_float[2][:, None]),
    )
    angles = chosen * inverse_freq[None, :]
    cosine = jnp.cos(angles)[:, None, :]
    sine_part = jnp.sin(angles)[:, None, :]
    first_half = vectors[..., :half_dim]
    second_half = vectors[..., half_dim:]
    return jnp.concatenate(
        [
            first_half * cosine - second_half * sine_part,
            second_half * cosine + first_half * sine_part,
        ],
        -1,
    )


def attend(turned, cache_keys, cache_values, fresh_keys, fresh_values, lengths):
    score_scale = 1.0 / math.sqrt(turned.shape[-1])
    slot_count = cache_keys.shape[1]
    cached = (
        jnp.einsum("rhd,rld->rhl", turned, cache_keys, preferred_element_type=jnp.float32)
        * score_scale
    )
    usable = lax.broadcasted_iota(jnp.int32, (turned.shape[0], slot_count), 1) < lengths[:, None]
    cached = jnp.where(usable[:, None, :], cached, -1e30)
    recent = (
        jnp.einsum("rhd,rnd->rhn", turned, fresh_keys, preferred_element_type=jnp.float32)
        * score_scale
    )
    scores = jnp.concatenate([cached, recent], -1)
    row_max = jnp.max(scores, -1, keepdims=True)
    shifted = jnp.exp(scores - row_max)
    weights = (shifted / jnp.sum(shifted, -1, keepdims=True)).astype(jnp.bfloat16)
    mixture = jnp.einsum(
        "rhl,rld->rhd", weights[..., :slot_count], cache_values, preferred_element_type=jnp.float32
    )
    mixture = mixture + jnp.einsum(
        "rhn,rnd->rhd", weights[..., slot_count:], fresh_values, preferred_element_type=jnp.float32
    )
    return mixture.astype(jnp.bfloat16)


def per_device(
    queries,
    new_kv,
    cache,
    lengths,
    positions,
    hidden,
    norm_gain,
    route_ids,
    route_weight,
    w_gate_up,
    w_down,
):
    step_count = queries.shape[0]
    requests = queries.shape[1]
    head_dim = cache.shape[-1]
    head_count = queries.shape[2] // head_dim
    turned_keys = [
        rotate(new_kv[step_at, 0][:, None, :].astype(jnp.float32), positions[step_at])[:, 0, :]
        for step_at in range(step_count)
    ]
    fresh_keys = jnp.stack(turned_keys, 1).astype(jnp.bfloat16)
    fresh_values = jnp.transpose(new_kv[:, 1], (1, 0, 2))
    attention = []
    for step_at in range(step_count):
        turned = rotate(
            queries[step_at].reshape(requests, head_count, head_dim).astype(jnp.float32),
            positions[step_at],
        )
        turned = turned.astype(jnp.bfloat16)
        mixture = attend(
            turned,
            cache[0],
            cache[1],
            fresh_keys[:, : step_at + 1],
            fresh_values[:, : step_at + 1],
            lengths,
        )
        attention.append(mixture.reshape(requests, head_count * head_dim))
    attention = jnp.stack(attention)
    owners = lax.axis_size("dp")
    groups = lax.axis_size("head")
    local_experts = w_down.shape[0]
    experts = owners * local_experts
    top_count = route_ids.shape[-1]
    slot_count = max(2, requests * top_count // experts)
    model_width = norm_gain.shape[0]
    hidden_part = w_down.shape[1]
    chunk = hidden.shape[-1]
    tokens = step_count * requests
    slots = step_count * slot_count

    slot_of = []
    for step_at in range(step_count):
        flat_ids = route_ids[step_at].reshape(-1)
        onehot = (
            flat_ids[:, None] == lax.broadcasted_iota(jnp.int32, (flat_ids.shape[0], experts), 1)
        ).astype(jnp.int32)
        rank_in = jnp.sum((jnp.cumsum(onehot, 0) - onehot) * onehot, 1)
        slot_of.append((flat_ids * slots + step_at * slot_count + rank_in).reshape(requests, top_count))
    slot_of = jnp.concatenate(slot_of, 0)
    slot_grid = lax.broadcasted_iota(jnp.int32, (experts, slots, tokens, top_count), 0) * slots + (
        lax.broadcasted_iota(jnp.int32, (experts, slots, tokens, top_count), 1)
    )
    hit = slot_grid == slot_of[None, None]
    placement = jnp.any(hit, 3).astype(jnp.bfloat16)
    own_rows = hidden.reshape(tokens, chunk)
    outgoing = jnp.einsum(
        "ejt,tf->ejf", placement, own_rows, preferred_element_type=jnp.float32
    ).astype(jnp.bfloat16)
    received = lax.all_to_all(outgoing, "dp", split_axis=0, concat_axis=0, tiled=True)
    received = received.reshape(experts * slots, chunk)
    assert groups == 4
    me = lax.axis_index("head")
    to_right = [(j, (j + 1) % groups) for j in range(groups)]
    to_left = [(j, (j - 1) % groups) for j in range(groups)]
    half = received.shape[0] // 2

    def ring_sum(terms, plus, side):
        rows = terms[0].shape[0]
        far_a = lax.ppermute(jnp.concatenate([terms[2][:half], side], 0), "head", to_right)
        far_b = lax.ppermute(jnp.concatenate([terms[2][half:], side], 0), "head", to_left)
        side_left, side_right = far_a[half:], far_b[half:]
        near_r = lax.ppermute(
            jnp.concatenate(
                [plus(terms[1][:half], far_a[:half]), terms[1][half:], side + side_left], 0
            ),
            "head",
            to_right,
        )
        near_l = lax.ppermute(
            jnp.concatenate([terms[3][:half], plus(terms[3][half:], far_b[:half])], 0),
            "head",
            to_left,
        )
        side_far = near_r[rows:]
        return plus(plus(terms[0], near_r[:rows]), near_l), side + side_right + side_far

    up_cols = w_gate_up[0]
    up_blocks = [lax.dynamic_slice_in_dim(up_cols, me * chunk, chunk, 0)]
    for k in range(1, groups):
        piece = lax.dynamic_slice_in_dim(up_cols, ((me - k) % groups) * chunk, chunk, 0)
        up_blocks.append(lax.ppermute(piece, "head", [(j, (j - k) % groups) for j in range(groups)]))
    down_rows = w_down[0]
    down_blocks = [lax.dynamic_slice_in_dim(down_rows, me * chunk, chunk, 1)]
    for k in range(1, groups):
        piece = lax.dynamic_slice_in_dim(down_rows, ((me - k) % groups) * chunk, chunk, 1)
        down_blocks.append(
            lax.ppermute(piece, "head", [(j, (j - k) % groups) for j in range(groups)])
        )
    own_gain = lax.dynamic_slice_in_dim(norm_gain, me * chunk, chunk).astype(jnp.float32)
    wide = received.astype(jnp.float32)
    up_width = 2 * hidden_part
    square_sums = jnp.sum(wide * wide, 1)
    side_rows = -(-square_sums.shape[0] // (8 * up_width)) * 8
    square_sums = jnp.pad(square_sums, (0, side_rows * up_width - square_sums.shape[0])).reshape(
        side_rows, up_width
    )
    scaled = (wide * own_gain[None, :]).astype(jnp.bfloat16)
    shares_of_up = jnp.einsum(
        "rf,kfc->krc", scaled, jnp.stack(up_blocks), preferred_element_type=jnp.float32
    )
    gate_up, square_sums = ring_sum(
        [shares_of_up[k] for k in range(groups)], lambda a, b: a + b, square_sums
    )
    mean_sq = square_sums.reshape(-1)[: received.shape[0]] / model_width
    gate_up = gate_up * lax.rsqrt(mean_sq + EPS)[:, None]
    activated = (jax.nn.silu(gate_up[:, :hidden_part]) * gate_up[:, hidden_part:]).astype(
        jnp.bfloat16
    )
    act_left = lax.ppermute(activated, "head", to_right)
    act_right = lax.ppermute(activated, "head", to_left)
    act_far = lax.ppermute(act_left, "head", to_right)
    act_blocks = [activated, act_right, act_far, act_left]
    summed = None
    for act_block, down_block in zip(act_blocks, down_blocks):
        part = (
            jnp.dot(act_block, down_block, preferred_element_type=jnp.float32)
            .astype(jnp.bfloat16)
            .astype(jnp.float32)
        )
        summed = part if summed is None else summed + part
    summed = summed.astype(jnp.bfloat16)
    returned = lax.all_to_all(
        summed.reshape(experts, slots, chunk), "dp", split_axis=0, concat_axis=0, tiled=True
    )

    shares = route_weight / jnp.sum(route_weight, -1, keepdims=True)
    combine = jnp.sum(
        jnp.where(hit, shares.reshape(1, 1, tokens, top_count), 0.0), 3
    )
    contrib = jnp.einsum(
        "ejt,ejf->tf",
        combine,
        returned.astype(jnp.float32),
        precision=lax.Precision.HIGHEST,
        preferred_element_type=jnp.float32,
    )
    layer_out = (own_rows.astype(jnp.float32) + contrib).astype(jnp.bfloat16)
    layer_out = layer_out.reshape(step_count, requests, chunk)
    return (attention, layer_out)


def solution(mesh):
    return jax.shard_map(
        per_device,
        mesh=mesh,
        in_specs=(
            P(None, "dp", "head"),
            P(None, None, "dp", "head"),
            P(None, "dp", None, "head"),
            P("dp"),
            P(None, None, "dp"),
            P(None, "dp", "head"),
            P(),
            P(None, "dp", None),
            P(None, "dp", None),
            P("dp", None, "head"),
            P("dp", "head", None),
        ),
        out_specs=(P(None, "dp", "head"), P(None, "dp", "head")),
        check_vma=False,
    )
```

```python
import math

import jax
import jax.numpy as jnp
from jax import lax
from jax.sharding import PartitionSpec as P

EPS = 1e-06
ROPE_BASE = 5000000.0


def rotate(vectors, pos_ids):
    head_size = vectors.shape[-1]
    half_dim = head_size // 2
    freq_index = jnp.arange(half_dim, dtype=jnp.int32)
    inverse_freq = jnp.exp(
        freq_index.astype(jnp.float32) * (-2.0 * math.log(ROPE_BASE) / head_size)
    )
    alternated = 60 * half_dim // 64
    axis_pick = jnp.where(freq_index < alternated, freq_index % 3, 0)
    pos_float = pos_ids.astype(jnp.float32)
    chosen = jnp.where(
        axis_pick[None, :] == 0,
        pos_float[0][:, None],
        jnp.where(axis_pick[None, :] == 1, pos_float[1][:, None], pos_float[2][:, None]),
    )
    angles = chosen * inverse_freq[None, :]
    cosine = jnp.cos(angles)[:, None, :]
    sine_part = jnp.sin(angles)[:, None, :]
    first_half = vectors[..., :half_dim]
    second_half = vectors[..., half_dim:]
    return jnp.concatenate(
        [
            first_half * cosine - second_half * sine_part,
            second_half * cosine + first_half * sine_part,
        ],
        -1,
    )


def attend(turned, cache_keys, cache_values, fresh_keys, fresh_values, lengths):
    score_scale = 1.0 / math.sqrt(turned.shape[-1])
    slot_count = cache_keys.shape[1]
    cached = (
        jnp.einsum("rhd,rld->rhl", turned, cache_keys, preferred_element_type=jnp.float32)
        * score_scale
    )
    usable = lax.broadcasted_iota(jnp.int32, (turned.shape[0], slot_count), 1) < lengths[:, None]
    cached = jnp.where(usable[:, None, :], cached, -1e30)
    recent = (
        jnp.einsum("rhd,rnd->rhn", turned, fresh_keys, preferred_element_type=jnp.float32)
        * score_scale
    )
    scores = jnp.concatenate([cached, recent], -1)
    row_max = jnp.max(scores, -1, keepdims=True)
    shifted = jnp.exp(scores - row_max)
    weights = (shifted / jnp.sum(shifted, -1, keepdims=True)).astype(jnp.bfloat16)
    mixture = jnp.einsum(
        "rhl,rld->rhd", weights[..., :slot_count], cache_values, preferred_element_type=jnp.float32
    )
    mixture = mixture + jnp.einsum(
        "rhn,rnd->rhd", weights[..., slot_count:], fresh_values, preferred_element_type=jnp.float32
    )
    return mixture.astype(jnp.bfloat16)


def per_device(
    queries,
    new_kv,
    cache,
    lengths,
    positions,
    hidden,
    norm_gain,
    route_ids,
    route_weight,
    w_gate_up,
    w_down,
):
    step_count = queries.shape[0]
    requests = queries.shape[1]
    head_dim = cache.shape[-1]
    head_count = queries.shape[2] // head_dim
    turned_keys = [
        rotate(new_kv[step_at, 0][:, None, :].astype(jnp.float32), positions[step_at])[:, 0, :]
        for step_at in range(step_count)
    ]
    fresh_keys = jnp.stack(turned_keys, 1).astype(jnp.bfloat16)
    fresh_values = jnp.transpose(new_kv[:, 1], (1, 0, 2))
    attention = []
    for step_at in range(step_count):
        turned = rotate(
            queries[step_at].reshape(requests, head_count, head_dim).astype(jnp.float32),
            positions[step_at],
        )
        turned = turned.astype(jnp.bfloat16)
        mixture = attend(
            turned,
            cache[0],
            cache[1],
            fresh_keys[:, : step_at + 1],
            fresh_values[:, : step_at + 1],
            lengths,
        )
        attention.append(mixture.reshape(requests, head_count * head_dim))
    attention = jnp.stack(attention)
    owners = lax.axis_size("dp")
    groups = lax.axis_size("head")
    local_experts = w_down.shape[0]
    experts = owners * local_experts
    top_count = route_ids.shape[-1]
    slot_count = max(2, requests * top_count // experts)
    model_width = norm_gain.shape[0]
    hidden_part = w_down.shape[1]
    chunk = hidden.shape[-1]
    tokens = step_count * requests
    slots = step_count * slot_count

    slot_of = []
    for step_at in range(step_count):
        flat_ids = route_ids[step_at].reshape(-1)
        onehot = (
            flat_ids[:, None] == lax.broadcasted_iota(jnp.int32, (flat_ids.shape[0], experts), 1)
        ).astype(jnp.int32)
        rank_in = jnp.sum((jnp.cumsum(onehot, 0) - onehot) * onehot, 1)
        slot_of.append((flat_ids * slots + step_at * slot_count + rank_in).reshape(requests, top_count))
    slot_of = jnp.concatenate(slot_of, 0)
    slot_grid = lax.broadcasted_iota(jnp.int32, (experts, slots, tokens, top_count), 0) * slots + (
        lax.broadcasted_iota(jnp.int32, (experts, slots, tokens, top_count), 1)
    )
    hit = slot_grid == slot_of[None, None]
    placement = jnp.any(hit, 3).astype(jnp.bfloat16)
    own_rows = hidden.reshape(tokens, chunk)
    outgoing = jnp.einsum(
        "ejt,tf->ejf", placement, own_rows, preferred_element_type=jnp.float32
    ).astype(jnp.bfloat16)
    received = lax.all_to_all(outgoing, "dp", split_axis=0, concat_axis=0, tiled=True)
    received = received.reshape(experts * slots, chunk)
    assert groups == 4
    me = lax.axis_index("head")
    to_right = [(j, (j + 1) % groups) for j in range(groups)]
    to_left = [(j, (j - 1) % groups) for j in range(groups)]
    half = received.shape[0] // 2

    def ring_sum(terms, plus, side):
        far_a = lax.ppermute(terms[2][:half], "head", to_right)
        far_b = lax.ppermute(terms[2][half:], "head", to_left)
        side_left = lax.ppermute(side, "head", to_right)
        side_right = lax.ppermute(side, "head", to_left)
        near_r = lax.ppermute(
            jnp.concatenate([plus(terms[1][:half], far_a), terms[1][half:]], 0), "head", to_right
        )
        near_l = lax.ppermute(
            jnp.concatenate([terms[3][:half], plus(terms[3][half:], far_b)], 0), "head", to_left
        )
        side_far = lax.ppermute(side + side_left, "head", to_right)
        return plus(plus(terms[0], near_r), near_l), side + side_right + side_far

    up_cols = w_gate_up[0]
    up_blocks = [lax.dynamic_slice_in_dim(up_cols, me * chunk, chunk, 0)]
    for k in range(1, groups):
        piece = lax.dynamic_slice_in_dim(up_cols, ((me - k) % groups) * chunk, chunk, 0)
        up_blocks.append(lax.ppermute(piece, "head", [(j, (j - k) % groups) for j in range(groups)]))
    down_rows = w_down[0]
    down_blocks = [lax.dynamic_slice_in_dim(down_rows, me * chunk, chunk, 1)]
    for k in range(1, groups):
        piece = lax.dynamic_slice_in_dim(down_rows, ((me - k) % groups) * chunk, chunk, 1)
        down_blocks.append(
            lax.ppermute(piece, "head", [(j, (j - k) % groups) for j in range(groups)])
        )
    received, up_blocks, down_blocks = lax.optimization_barrier((received, up_blocks, down_blocks))
    own_gain = lax.dynamic_slice_in_dim(norm_gain, me * chunk, chunk).astype(jnp.float32)
    wide = received.astype(jnp.float32)
    square_sums = jnp.sum(wide * wide, 1)
    scaled = (wide * own_gain[None, :]).astype(jnp.bfloat16)
    shares_of_up = jnp.einsum(
        "rf,kfc->krc", scaled, jnp.stack(up_blocks), preferred_element_type=jnp.float32
    )
    gate_up, square_sums = ring_sum(
        [shares_of_up[k] for k in range(groups)], lambda a, b: a + b, square_sums
    )
    mean_sq = square_sums / model_width
    gate_up = gate_up * lax.rsqrt(mean_sq + EPS)[:, None]
    activated = (jax.nn.silu(gate_up[:, :hidden_part]) * gate_up[:, hidden_part:]).astype(
        jnp.bfloat16
    )
    act_left = lax.ppermute(activated, "head", to_right)
    act_right = lax.ppermute(activated, "head", to_left)
    act_far = lax.ppermute(act_left, "head", to_right)
    act_blocks = [activated, act_right, act_far, act_left]
    summed = None
    for act_block, down_block in zip(act_blocks, down_blocks):
        part = (
            jnp.dot(act_block, down_block, preferred_element_type=jnp.float32)
            .astype(jnp.bfloat16)
            .astype(jnp.float32)
        )
        summed = part if summed is None else summed + part
    summed = summed.astype(jnp.bfloat16)
    returned = lax.all_to_all(
        summed.reshape(experts, slots, chunk), "dp", split_axis=0, concat_axis=0, tiled=True
    )

    shares = route_weight / jnp.sum(route_weight, -1, keepdims=True)
    combine = jnp.sum(
        jnp.where(hit, shares.reshape(1, 1, tokens, top_count), 0.0), 3
    )
    contrib = jnp.einsum(
        "ejt,ejf->tf",
        combine,
        returned.astype(jnp.float32),
        precision=lax.Precision.HIGHEST,
        preferred_element_type=jnp.float32,
    )
    layer_out = (own_rows.astype(jnp.float32) + contrib).astype(jnp.bfloat16)
    layer_out = layer_out.reshape(step_count, requests, chunk)
    return (attention, layer_out)


def solution(mesh):
    return jax.shard_map(
        per_device,
        mesh=mesh,
        in_specs=(
            P(None, "dp", "head"),
            P(None, None, "dp", "head"),
            P(None, "dp", None, "head"),
            P("dp"),
            P(None, None, "dp"),
            P(None, "dp", "head"),
            P(),
            P(None, "dp", None),
            P(None, "dp", None),
            P("dp", None, "head"),
            P("dp", "head", None),
        ),
        out_specs=(P(None, "dp", "head"), P(None, "dp", "head")),
        check_vma=False,
    )
```

```python
import math

import jax
import jax.numpy as jnp
from jax import lax
from jax.sharding import PartitionSpec as P

EPS = 1e-06
ROPE_BASE = 5000000.0


def rotate(vectors, pos_ids):
    head_size = vectors.shape[-1]
    half_dim = head_size // 2
    freq_index = jnp.arange(half_dim, dtype=jnp.int32)
    inverse_freq = jnp.exp(
        freq_index.astype(jnp.float32) * (-2.0 * math.log(ROPE_BASE) / head_size)
    )
    alternated = 60 * half_dim // 64
    axis_pick = jnp.where(freq_index < alternated, freq_index % 3, 0)
    pos_float = pos_ids.astype(jnp.float32)
    chosen = jnp.where(
        axis_pick[None, :] == 0,
        pos_float[0][:, None],
        jnp.where(axis_pick[None, :] == 1, pos_float[1][:, None], pos_float[2][:, None]),
    )
    angles = chosen * inverse_freq[None, :]
    cosine = jnp.cos(angles)[:, None, :]
    sine_part = jnp.sin(angles)[:, None, :]
    first_half = vectors[..., :half_dim]
    second_half = vectors[..., half_dim:]
    return jnp.concatenate(
        [
            first_half * cosine - second_half * sine_part,
            second_half * cosine + first_half * sine_part,
        ],
        -1,
    )


def attend(turned, cache_keys, cache_values, fresh_keys, fresh_values, lengths):
    score_scale = 1.0 / math.sqrt(turned.shape[-1])
    slot_count = cache_keys.shape[1]
    cached = (
        jnp.einsum("rhd,rld->rhl", turned, cache_keys, preferred_element_type=jnp.float32)
        * score_scale
    )
    usable = lax.broadcasted_iota(jnp.int32, (turned.shape[0], slot_count), 1) < lengths[:, None]
    cached = jnp.where(usable[:, None, :], cached, -1e30)
    recent = (
        jnp.einsum("rhd,rnd->rhn", turned, fresh_keys, preferred_element_type=jnp.float32)
        * score_scale
    )
    scores = jnp.concatenate([cached, recent], -1)
    row_max = jnp.max(scores, -1, keepdims=True)
    shifted = jnp.exp(scores - row_max)
    weights = (shifted / jnp.sum(shifted, -1, keepdims=True)).astype(jnp.bfloat16)
    mixture = jnp.einsum(
        "rhl,rld->rhd", weights[..., :slot_count], cache_values, preferred_element_type=jnp.float32
    )
    mixture = mixture + jnp.einsum(
        "rhn,rnd->rhd", weights[..., slot_count:], fresh_values, preferred_element_type=jnp.float32
    )
    return mixture.astype(jnp.bfloat16)


def per_device(
    queries,
    new_kv,
    cache,
    lengths,
    positions,
    hidden,
    norm_gain,
    route_ids,
    route_weight,
    w_gate_up,
    w_down,
):
    step_count = queries.shape[0]
    requests = queries.shape[1]
    head_dim = cache.shape[-1]
    head_count = queries.shape[2] // head_dim
    turned_keys = [
        rotate(new_kv[step_at, 0][:, None, :].astype(jnp.float32), positions[step_at])[:, 0, :]
        for step_at in range(step_count)
    ]
    fresh_keys = jnp.stack(turned_keys, 1).astype(jnp.bfloat16)
    fresh_values = jnp.transpose(new_kv[:, 1], (1, 0, 2))
    attention = []
    for step_at in range(step_count):
        turned = rotate(
            queries[step_at].reshape(requests, head_count, head_dim).astype(jnp.float32),
            positions[step_at],
        )
        turned = turned.astype(jnp.bfloat16)
        mixture = attend(
            turned,
            cache[0],
            cache[1],
            fresh_keys[:, : step_at + 1],
            fresh_values[:, : step_at + 1],
            lengths,
        )
        attention.append(mixture.reshape(requests, head_count * head_dim))
    attention = jnp.stack(attention)
    owners = lax.axis_size("dp")
    groups = lax.axis_size("head")
    local_experts = w_down.shape[0]
    experts = owners * local_experts
    top_count = route_ids.shape[-1]
    slot_count = max(2, requests * top_count // experts)
    model_width = norm_gain.shape[0]
    hidden_part = w_down.shape[1]
    chunk = hidden.shape[-1]
    tokens = step_count * requests
    slots = step_count * slot_count

    slot_of = []
    for step_at in range(step_count):
        flat_ids = route_ids[step_at].reshape(-1)
        onehot = (
            flat_ids[:, None] == lax.broadcasted_iota(jnp.int32, (flat_ids.shape[0], experts), 1)
        ).astype(jnp.int32)
        rank_in = jnp.sum((jnp.cumsum(onehot, 0) - onehot) * onehot, 1)
        slot_of.append((flat_ids * slots + step_at * slot_count + rank_in).reshape(requests, top_count))
    slot_of = jnp.concatenate(slot_of, 0)
    slot_grid = lax.broadcasted_iota(jnp.int32, (experts, slots, tokens, top_count), 0) * slots + (
        lax.broadcasted_iota(jnp.int32, (experts, slots, tokens, top_count), 1)
    )
    hit = slot_grid == slot_of[None, None]
    placement = jnp.any(hit, 3).astype(jnp.bfloat16)
    own_rows = hidden.reshape(tokens, chunk)
    outgoing = jnp.einsum(
        "ejt,tf->ejf", placement, own_rows, preferred_element_type=jnp.float32
    ).astype(jnp.bfloat16)
    received = lax.all_to_all(outgoing, "dp", split_axis=0, concat_axis=0, tiled=True)
    received = received.reshape(experts * slots, chunk)
    assert groups == 4
    me = lax.axis_index("head")
    to_right = [(j, (j + 1) % groups) for j in range(groups)]
    to_left = [(j, (j - 1) % groups) for j in range(groups)]
    half = received.shape[0] // 2

    def ring_sum(terms, plus, side):
        far_a = lax.ppermute(terms[2][:half], "head", to_right)
        far_b = lax.ppermute(terms[2][half:], "head", to_left)
        near_r = lax.ppermute(
            jnp.concatenate([plus(terms[1][:half], far_a), terms[1][half:]], 0), "head", to_right
        )
        near_l = lax.ppermute(
            jnp.concatenate([terms[3][:half], plus(terms[3][half:], far_b)], 0), "head", to_left
        )
        return plus(plus(terms[0], near_r), near_l), lax.psum(side, "head")

    up_cols = w_gate_up[0]
    up_blocks = [lax.dynamic_slice_in_dim(up_cols, me * chunk, chunk, 0)]
    for k in range(1, groups):
        piece = lax.dynamic_slice_in_dim(up_cols, ((me - k) % groups) * chunk, chunk, 0)
        up_blocks.append(lax.ppermute(piece, "head", [(j, (j - k) % groups) for j in range(groups)]))
    down_rows = w_down[0]
    down_blocks = [lax.dynamic_slice_in_dim(down_rows, me * chunk, chunk, 1)]
    for k in range(1, groups):
        piece = lax.dynamic_slice_in_dim(down_rows, ((me - k) % groups) * chunk, chunk, 1)
        down_blocks.append(
            lax.ppermute(piece, "head", [(j, (j - k) % groups) for j in range(groups)])
        )
    own_gain = lax.dynamic_slice_in_dim(norm_gain, me * chunk, chunk).astype(jnp.float32)
    wide = received.astype(jnp.float32)
    square_sums = jnp.sum(wide * wide, 1)
    scaled = (wide * own_gain[None, :]).astype(jnp.bfloat16)
    shares_of_up = jnp.einsum(
        "rf,kfc->krc", scaled, jnp.stack(up_blocks), preferred_element_type=jnp.float32
    )
    gate_up, square_sums = ring_sum(
        [shares_of_up[k] for k in range(groups)], lambda a, b: a + b, square_sums
    )
    mean_sq = square_sums / model_width
    gate_up = gate_up * lax.rsqrt(mean_sq + EPS)[:, None]
    activated = (jax.nn.silu(gate_up[:, :hidden_part]) * gate_up[:, hidden_part:]).astype(
        jnp.bfloat16
    )
    act_left = lax.ppermute(activated, "head", to_right)
    act_right = lax.ppermute(activated, "head", to_left)
    act_far = lax.ppermute(act_left, "head", to_right)
    act_blocks = [activated, act_right, act_far, act_left]
    summed = None
    for act_block, down_block in zip(act_blocks, down_blocks):
        part = (
            jnp.dot(act_block, down_block, preferred_element_type=jnp.float32)
            .astype(jnp.bfloat16)
            .astype(jnp.float32)
        )
        summed = part if summed is None else summed + part
    summed = summed.astype(jnp.bfloat16)
    returned = lax.all_to_all(
        summed.reshape(experts, slots, chunk), "dp", split_axis=0, concat_axis=0, tiled=True
    )

    shares = route_weight / jnp.sum(route_weight, -1, keepdims=True)
    combine = jnp.sum(
        jnp.where(hit, shares.reshape(1, 1, tokens, top_count), 0.0), 3
    )
    contrib = jnp.einsum(
        "ejt,ejf->tf",
        combine,
        returned.astype(jnp.float32),
        precision=lax.Precision.HIGHEST,
        preferred_element_type=jnp.float32,
    )
    layer_out = (own_rows.astype(jnp.float32) + contrib).astype(jnp.bfloat16)
    layer_out = layer_out.reshape(step_count, requests, chunk)
    return (attention, layer_out)


def solution(mesh):
    return jax.shard_map(
        per_device,
        mesh=mesh,
        in_specs=(
            P(None, "dp", "head"),
            P(None, None, "dp", "head"),
            P(None, "dp", None, "head"),
            P("dp"),
            P(None, None, "dp"),
            P(None, "dp", "head"),
            P(),
            P(None, "dp", None),
            P(None, "dp", None),
            P("dp", None, "head"),
            P("dp", "head", None),
        ),
        out_specs=(P(None, "dp", "head"), P(None, "dp", "head")),
        check_vma=False,
    )
```

```python
import math

import jax
import jax.numpy as jnp
from jax import lax
from jax.sharding import PartitionSpec as P

EPS = 1e-06
ROPE_BASE = 5000000.0


def rotate(vectors, pos_ids):
    head_size = vectors.shape[-1]
    half_dim = head_size // 2
    freq_index = jnp.arange(half_dim, dtype=jnp.int32)
    inverse_freq = jnp.exp(
        freq_index.astype(jnp.float32) * (-2.0 * math.log(ROPE_BASE) / head_size)
    )
    alternated = 60 * half_dim // 64
    axis_pick = jnp.where(freq_index < alternated, freq_index % 3, 0)
    pos_float = pos_ids.astype(jnp.float32)
    chosen = jnp.where(
        axis_pick[None, :] == 0,
        pos_float[0][:, None],
        jnp.where(axis_pick[None, :] == 1, pos_float[1][:, None], pos_float[2][:, None]),
    )
    angles = chosen * inverse_freq[None, :]
    cosine = jnp.cos(angles)[:, None, :]
    sine_part = jnp.sin(angles)[:, None, :]
    first_half = vectors[..., :half_dim]
    second_half = vectors[..., half_dim:]
    return jnp.concatenate(
        [
            first_half * cosine - second_half * sine_part,
            second_half * cosine + first_half * sine_part,
        ],
        -1,
    )


def attend(turned, cache_keys, cache_values, fresh_keys, fresh_values, lengths):
    score_scale = 1.0 / math.sqrt(turned.shape[-1])
    slot_count = cache_keys.shape[1]
    cached = (
        jnp.einsum("rhd,rld->rhl", turned, cache_keys, preferred_element_type=jnp.float32)
        * score_scale
    )
    usable = lax.broadcasted_iota(jnp.int32, (turned.shape[0], slot_count), 1) < lengths[:, None]
    cached = jnp.where(usable[:, None, :], cached, -1e30)
    recent = (
        jnp.einsum("rhd,rnd->rhn", turned, fresh_keys, preferred_element_type=jnp.float32)
        * score_scale
    )
    scores = jnp.concatenate([cached, recent], -1)
    row_max = jnp.max(scores, -1, keepdims=True)
    shifted = jnp.exp(scores - row_max)
    weights = (shifted / jnp.sum(shifted, -1, keepdims=True)).astype(jnp.bfloat16)
    mixture = jnp.einsum(
        "rhl,rld->rhd", weights[..., :slot_count], cache_values, preferred_element_type=jnp.float32
    )
    mixture = mixture + jnp.einsum(
        "rhn,rnd->rhd", weights[..., slot_count:], fresh_values, preferred_element_type=jnp.float32
    )
    return mixture.astype(jnp.bfloat16)


def per_device(
    queries,
    new_kv,
    cache,
    lengths,
    positions,
    hidden,
    norm_gain,
    route_ids,
    route_weight,
    w_gate_up,
    w_down,
):
    step_count = queries.shape[0]
    requests = queries.shape[1]
    head_dim = cache.shape[-1]
    head_count = queries.shape[2] // head_dim
    turned_keys = [
        rotate(new_kv[step_at, 0][:, None, :].astype(jnp.float32), positions[step_at])[:, 0, :]
        for step_at in range(step_count)
    ]
    fresh_keys = jnp.stack(turned_keys, 1).astype(jnp.bfloat16)
    fresh_values = jnp.transpose(new_kv[:, 1], (1, 0, 2))
    attention = []
    for step_at in range(step_count):
        turned = rotate(
            queries[step_at].reshape(requests, head_count, head_dim).astype(jnp.float32),
            positions[step_at],
        )
        turned = turned.astype(jnp.bfloat16)
        mixture = attend(
            turned,
            cache[0],
            cache[1],
            fresh_keys[:, : step_at + 1],
            fresh_values[:, : step_at + 1],
            lengths,
        )
        attention.append(mixture.reshape(requests, head_count * head_dim))
    attention = jnp.stack(attention)
    owners = lax.axis_size("dp")
    groups = lax.axis_size("head")
    local_experts = w_down.shape[0]
    experts = owners * local_experts
    top_count = route_ids.shape[-1]
    slot_count = max(2, requests * top_count // experts)
    model_width = norm_gain.shape[0]
    hidden_part = w_down.shape[1]
    chunk = hidden.shape[-1]
    tokens = step_count * requests
    slots = step_count * slot_count

    slot_of = []
    for step_at in range(step_count):
        flat_ids = route_ids[step_at].reshape(-1)
        onehot = (
            flat_ids[:, None] == lax.broadcasted_iota(jnp.int32, (flat_ids.shape[0], experts), 1)
        ).astype(jnp.int32)
        rank_in = jnp.sum((jnp.cumsum(onehot, 0) - onehot) * onehot, 1)
        slot_of.append((flat_ids * slots + step_at * slot_count + rank_in).reshape(requests, top_count))
    slot_of = jnp.concatenate(slot_of, 0)
    slot_grid = lax.broadcasted_iota(jnp.int32, (experts, slots, tokens, top_count), 0) * slots + (
        lax.broadcasted_iota(jnp.int32, (experts, slots, tokens, top_count), 1)
    )
    hit = slot_grid == slot_of[None, None]
    placement = jnp.any(hit, 3).astype(jnp.bfloat16)
    own_rows = hidden.reshape(tokens, chunk)
    outgoing = jnp.einsum(
        "ejt,tf->ejf", placement, own_rows, preferred_element_type=jnp.float32
    ).astype(jnp.bfloat16)
    received = lax.all_to_all(outgoing, "dp", split_axis=0, concat_axis=0, tiled=True)
    received = received.reshape(experts * slots, chunk)
    assert groups == 4
    me = lax.axis_index("head")
    to_right = [(j, (j + 1) % groups) for j in range(groups)]
    to_left = [(j, (j - 1) % groups) for j in range(groups)]
    half = received.shape[0] // 2

    def ring_sum(terms, plus, side):
        far = lax.ppermute(terms[2], "head", to_right)
        near_r = lax.ppermute(plus(terms[1], far), "head", to_right)
        near_l = lax.ppermute(terms[3], "head", to_left)
        return plus(plus(terms[0], near_r), near_l), lax.psum(side, "head")

    up_cols = w_gate_up[0]
    up_blocks = [lax.dynamic_slice_in_dim(up_cols, me * chunk, chunk, 0)]
    for k in range(1, groups):
        piece = lax.dynamic_slice_in_dim(up_cols, ((me - k) % groups) * chunk, chunk, 0)
        up_blocks.append(lax.ppermute(piece, "head", [(j, (j - k) % groups) for j in range(groups)]))
    down_rows = w_down[0]
    down_blocks = [lax.dynamic_slice_in_dim(down_rows, me * chunk, chunk, 1)]
    for k in range(1, groups):
        piece = lax.dynamic_slice_in_dim(down_rows, ((me - k) % groups) * chunk, chunk, 1)
        down_blocks.append(
            lax.ppermute(piece, "head", [(j, (j - k) % groups) for j in range(groups)])
        )
    own_gain = lax.dynamic_slice_in_dim(norm_gain, me * chunk, chunk).astype(jnp.float32)
    wide = received.astype(jnp.float32)
    square_sums = jnp.sum(wide * wide, 1)
    scaled = (wide * own_gain[None, :]).astype(jnp.bfloat16)
    shares_of_up = jnp.einsum(
        "rf,kfc->krc", scaled, jnp.stack(up_blocks), preferred_element_type=jnp.float32
    )
    gate_up, square_sums = ring_sum(
        [shares_of_up[k] for k in range(groups)], lambda a, b: a + b, square_sums
    )
    mean_sq = square_sums / model_width
    gate_up = gate_up * lax.rsqrt(mean_sq + EPS)[:, None]
    activated = (jax.nn.silu(gate_up[:, :hidden_part]) * gate_up[:, hidden_part:]).astype(
        jnp.bfloat16
    )
    act_left = lax.ppermute(activated, "head", to_right)
    act_right = lax.ppermute(activated, "head", to_left)
    act_far = lax.ppermute(act_left, "head", to_right)
    act_blocks = [activated, act_right, act_far, act_left]
    summed = None
    for act_block, down_block in zip(act_blocks, down_blocks):
        part = (
            jnp.dot(act_block, down_block, preferred_element_type=jnp.float32)
            .astype(jnp.bfloat16)
            .astype(jnp.float32)
        )
        summed = part if summed is None else summed + part
    summed = summed.astype(jnp.bfloat16)
    returned = lax.all_to_all(
        summed.reshape(experts, slots, chunk), "dp", split_axis=0, concat_axis=0, tiled=True
    )

    shares = route_weight / jnp.sum(route_weight, -1, keepdims=True)
    combine = jnp.sum(
        jnp.where(hit, shares.reshape(1, 1, tokens, top_count), 0.0), 3
    )
    contrib = jnp.einsum(
        "ejt,ejf->tf",
        combine,
        returned.astype(jnp.float32),
        precision=lax.Precision.HIGHEST,
        preferred_element_type=jnp.float32,
    )
    layer_out = (own_rows.astype(jnp.float32) + contrib).astype(jnp.bfloat16)
    layer_out = layer_out.reshape(step_count, requests, chunk)
    return (attention, layer_out)


def solution(mesh):
    return jax.shard_map(
        per_device,
        mesh=mesh,
        in_specs=(
            P(None, "dp", "head"),
            P(None, None, "dp", "head"),
            P(None, "dp", None, "head"),
            P("dp"),
            P(None, None, "dp"),
            P(None, "dp", "head"),
            P(),
            P(None, "dp", None),
            P(None, "dp", None),
            P("dp", None, "head"),
            P("dp", "head", None),
        ),
        out_specs=(P(None, "dp", "head"), P(None, "dp", "head")),
        check_vma=False,
    )
```
